256 devices in a mesh: mem: 8 (over x, y_hi), lat: 32 (over y_lo, z, core).
Axes of the slice: x: 4, y: 4 (y_hi: 2, y_lo: 2; y = y_hi * 2 + y_lo), z: 8, core: 2. Of those that a mesh axis runs over, the one named last changes fastest.
Arguments:
- cotangent: bfloat16 [8, 3, 4, 1024, 4096], P('mem', None, None, 'lat'), may hold values from -6 to 6
- legendre: bfloat16 [704, 2, 352, 512], P('lat', None, None, 'mem'), may hold values from -0.25 to 0.25
- wave_order: int32 [704], replicated, may hold values from 0 to 703, each once
- mode_depth: float32 [4], replicated, may hold values from 0.5 to 20
- diffusion: float32 [4], replicated, may hold values from 0.5 to 8
- quad_weights: float32 [512], replicated, may hold values from 0.25 to 2.5
Outputs:
- adjoint: bfloat16 [8, 3, 4, 1024, 4096], P('mem', None, None, 'lat')
The draws below stay inside these ranges and needn't reach their ends.
Inputs may be any that keep to these rules, and one draw needn't show every extreme that they name: `wave_order`: each zonal wavenumber 0 to 703 appears exactly once; legendre's first index follows this order.
All inputs are finite; a program needn't handle non-finite values.
Results may differ from the reference program's by a relative error of at most 0.0076.
Values may be sent and summed in bfloat16 or wider, within the bound.
No kernel may reach another device: no remote copies, remote signals or barrier semaphores. Data moves between devices by JAX's collectives and lax.ppermute only.
A program may use at most 192 MiB of HBM per device.

```python
import math
import jax
import jax.numpy as jnp
from jax import lax

NLON = 4096
NLAT = 1024
WAVES = 704
DEGREES = 704
MODES = 4
MEMBERS = 8
NLATH = 512


def steps_of(stream_key, shape, cuts, least, high):
    factor_of = 1.0
    for dim, parts in cuts:
        steps = jax.random.uniform(jax.random.fold_in(jax.random.fold_in(stream_key, 6), dim), (parts,), jnp.float32, least / len(cuts), high / len(cuts))
        factor_of = factor_of * jnp.repeat(jnp.exp(steps), shape[dim] // parts).reshape((-1,) + (1,) * (len(shape) - 1 - dim))
    return factor_of


def centred(stream_key, extent, deviation, most, split=(), kind=jnp.bfloat16):
    drawn = deviation * jax.random.normal(stream_key, extent, jnp.float32)
    if split:
        drawn = drawn * steps_of(stream_key, extent, split, -0.22, 0.18)
    return jnp.clip(drawn, -most, most).astype(kind)


def setup_inputs(seed: int = 0) -> dict:
    key_list = jax.random.split(jax.random.key(seed), 7)
    return {
        "cotangent": centred(key_list[0], (MEMBERS, 3, MODES, NLAT, NLON), 1.0, 6.0, ((0, 8), (3, 32))),
        "legendre": centred(key_list[1], (WAVES, 2, DEGREES // 2, NLATH), NLATH ** -0.5, 0.25, ((0, 32), (3, 8))),
        "wave_order": jax.random.permutation(key_list[2], WAVES).astype(jnp.int32),
        "mode_depth": jnp.clip(jnp.exp(jax.random.uniform(key_list[3], (MODES,), jnp.float32, math.log(0.5), math.log(20.0))), 0.5, 20.0),
        "diffusion": jnp.clip(jnp.exp(jax.random.uniform(key_list[4], (MODES,), jnp.float32, math.log(0.5), math.log(8.0))), 0.5, 8.0),
        "quad_weights": jnp.clip(jnp.exp(jax.random.uniform(key_list[5], (NLATH,), jnp.float32, math.log(0.25), math.log(2.5))), 0.25, 2.5),
    }


def fourier_table(wave_order, lon_count):
    wave_ids = jnp.repeat(wave_order, 2)
    parity = jnp.arange(wave_ids.shape[0], dtype=jnp.int32) % 2
    longitude = jnp.arange(lon_count, dtype=jnp.int32)[:, None]
    phases = (longitude * wave_ids[None, :]) % lon_count
    angles = phases.astype(jnp.float32) * jnp.float32(2.0 * math.pi / lon_count)
    values = jnp.where(parity[None, :] == 0, jnp.cos(angles), -jnp.sin(angles))
    return values.astype(jnp.bfloat16), wave_ids


def implicit(spectral, degree, top_degree, mode_depth, diffusion):
    count_waves, half_deg, pieces, channels = spectral.shape
    levels = mode_depth.shape[0]
    values = spectral.reshape(count_waves, half_deg, pieces, 3, levels)
    degree_f = degree.astype(jnp.float32)
    scaled = (degree_f * (degree_f + 1.0) / (top_degree * (top_degree + 1.0)))[:, :, None, None]
    vorticity = values[:, :, :, 0] / (1.0 + diffusion * scaled * scaled)
    damping = 1.0 / (1.0 + mode_depth * scaled)
    divergence = damping * (values[:, :, :, 1] - mode_depth * values[:, :, :, 2])
    height = damping * (scaled * values[:, :, :, 1] + values[:, :, :, 2])
    joined = jnp.stack([vorticity, divergence, height], axis=3)
    return joined.reshape(count_waves, half_deg, pieces, channels).astype(jnp.bfloat16)


def widen(values):
    return lax.optimization_barrier(values).astype(jnp.float32)


def one_member(member_field, legendre, wave_order, mode_depth, diffusion, quad_weights):
    highest = lax.Precision.HIGHEST
    fields, levels, lat_count, lon_count = member_field.shape
    half_lat = lat_count // 2
    total_waves = wave_order.shape[0]
    half_deg = legendre.shape[2]
    channels = fields * levels
    fourier, wave_ids = fourier_table(wave_order, lon_count)
    table_wide = fourier.astype(jnp.float32)
    flattened = member_field.reshape(channels * lat_count, lon_count).astype(jnp.float32)
    coeffs = jnp.dot(flattened, table_wide, precision=highest)
    factor = jnp.where(wave_ids == 0, 1.0, 2.0).astype(jnp.float32)
    coeffs = (coeffs * factor[None, :]).astype(jnp.bfloat16)
    coeffs = widen(coeffs).T.reshape(total_waves, 2, channels, lat_count)
    northern = coeffs[..., :half_lat]
    southern = coeffs[..., half_lat:]
    even_part = widen((northern + southern).astype(jnp.bfloat16))
    odd_part = widen((northern - southern).astype(jnp.bfloat16))
    basis_wide = legendre.astype(jnp.float32)
    analysed_even = jnp.einsum("mil,mqcl->miqc", basis_wide[:, 0], even_part, precision=highest)
    analysed_odd = jnp.einsum("mil,mqcl->miqc", basis_wide[:, 1], odd_part, precision=highest)
    degree_base = 2 * jnp.arange(half_deg, dtype=jnp.int32)[None, :] + wave_order[:, None]
    top_degree = float(total_waves + 2 * half_deg - 2)
    spectral_even = widen(implicit(analysed_even, degree_base, top_degree, mode_depth, diffusion))
    spectral_odd = widen(implicit(analysed_odd, degree_base + 1, top_degree, mode_depth, diffusion))
    synth_even = jnp.einsum("mil,miqc->mqcl", basis_wide[:, 0], spectral_even, precision=highest)
    synth_odd = jnp.einsum("mil,miqc->mqcl", basis_wide[:, 1], spectral_odd, precision=highest)
    weights = quad_weights[None, None, None, :]
    gridded = jnp.concatenate([weights * (synth_even + synth_odd), weights * (synth_even - synth_odd)], axis=3)
    gridded = widen(gridded.astype(jnp.bfloat16)).reshape(2 * total_waves, channels * lat_count)
    result = jnp.dot(gridded.T, table_wide.T, precision=highest) * (1.0 / lon_count)
    return result.astype(jnp.bfloat16).reshape(fields, levels, lat_count, lon_count)


def reference(cotangent, legendre, wave_order, mode_depth, diffusion, quad_weights):
    def single(member_field):
        return one_member(member_field, legendre, wave_order, mode_depth, diffusion, quad_weights)

    return lax.map(single, cotangent)
```

```python
import math

import jax
import jax.numpy as jnp
from jax import lax
from jax.sharding import PartitionSpec as P


def fourier_table(wave_order, lon_count):
    inner = 1 << (lon_count.bit_length() - 1) // 2
    outer = lon_count // inner
    step = jnp.float32(2.0 * math.pi / lon_count)
    waves = wave_order[None, :]
    phase_a = (jnp.arange(outer, dtype=jnp.int32)[:, None] * inner * waves) % lon_count
    phase_b = (jnp.arange(inner, dtype=jnp.int32)[:, None] * waves) % lon_count
    angle_a = phase_a.astype(jnp.float32) * step
    angle_b = phase_b.astype(jnp.float32) * step
    cos_a, sin_a = jnp.cos(angle_a)[:, None, :], jnp.sin(angle_a)[:, None, :]
    cos_b, sin_b = jnp.cos(angle_b)[None, :, :], jnp.sin(angle_b)[None, :, :]
    cosine = (cos_a * cos_b - sin_a * sin_b).reshape(lon_count, -1)
    sine = (sin_a * cos_b + cos_a * sin_b).reshape(lon_count, -1)
    table = jnp.concatenate([cosine, -sine], axis=1).astype(jnp.bfloat16)
    return lax.optimization_barrier(table)


def implicit(values, degree, top_degree, mode_depth, diffusion):
    shape = values.shape
    levels = mode_depth.shape[0]
    values = values.reshape(shape[:-1] + (3, levels))
    degree_f = degree.astype(jnp.float32)
    scaled = (degree_f * (degree_f + 1.0) / (top_degree * (top_degree + 1.0)))[
        :, :, :, None, None, None
    ]
    vorticity = values[..., 0, :] / (1.0 + diffusion * scaled * scaled)
    damping = 1.0 / (1.0 + mode_depth * scaled)
    divergence = damping * (values[..., 1, :] - mode_depth * values[..., 2, :])
    height = damping * (scaled * values[..., 1, :] + values[..., 2, :])
    joined = jnp.stack([vorticity, divergence, height], axis=-2)
    return joined.reshape(shape).astype(jnp.bfloat16)


def shards(cotangent, legendre, wave_order, mode_depth, diffusion, quad_weights):
    members, fields, levels, band_rows, lon_count = cotangent.shape
    lat_count = lax.axis_size("lat")
    mem_count = lax.axis_size("mem")
    half_count = lat_count // 2
    total_waves = wave_order.shape[0]
    count_waves = total_waves // lat_count
    group = -(-count_waves // mem_count)
    padded = group * mem_count
    half_deg = legendre.shape[2]
    slab = legendre.shape[3]
    half_lat = slab * mem_count
    channels = fields * levels
    top_degree = float(total_waves + 2 * half_deg - 2)
    lat_id = lax.axis_index("lat")
    mem_id = lax.axis_index("mem")

    basis = jnp.pad(legendre, ((0, padded - count_waves), (0, 0), (0, 0), (0, 0)))
    basis = basis.reshape(mem_count, group, 2, half_deg, slab)
    basis = lax.all_to_all(basis, "mem", 0, 0, tiled=True)
    basis = jnp.transpose(basis, (1, 2, 3, 0, 4)).reshape(group, 2, half_deg, half_lat)

    table = fourier_table(wave_order, lon_count)
    flattened = cotangent.reshape(channels * band_rows, lon_count)
    factor = jnp.where(wave_order == 0, 1.0, 2.0).astype(jnp.float32)
    factor = jnp.concatenate([factor, factor])
    coeffs = lax.dot_general(
        table, flattened, (((0,), (1,)), ((), ())), preferred_element_type=jnp.float32
    )
    coeffs = (coeffs * factor[:, None]).astype(jnp.bfloat16)
    coeffs = coeffs.reshape(2, lat_count, count_waves, channels * band_rows)
    received = lax.all_to_all(coeffs, "lat", 1, 1, tiled=True)
    received = received.reshape(2, lat_count, count_waves, channels, band_rows)
    northern = received[:, :half_count].astype(jnp.float32)
    southern = received[:, half_count:].astype(jnp.float32)
    even_part = (northern + southern).astype(jnp.bfloat16)
    odd_part = (northern - southern).astype(jnp.bfloat16)
    parts = jnp.stack([even_part, odd_part], axis=0)
    parts = jnp.pad(parts, ((0, 0), (0, 0), (0, 0), (0, padded - count_waves), (0, 0), (0, 0)))
    parts = jnp.transpose(parts, (3, 0, 1, 4, 2, 5)).reshape(
        mem_count, group, 2, 2, channels, half_lat
    )
    parts = lax.all_to_all(parts, "mem", 0, 0, tiled=True)

    analysed = jnp.einsum(
        "kpiy,ekpqcy->kpieqc", basis, parts, preferred_element_type=jnp.float32
    )
    local = mem_id * group + jnp.arange(group, dtype=jnp.int32)
    index = jnp.minimum(lat_id * count_waves + local, total_waves - 1)
    own_waves = jnp.take(wave_order, index)
    degree = (
        own_waves[:, None, None]
        + 2 * jnp.arange(half_deg, dtype=jnp.int32)[None, None, :]
        + jnp.arange(2, dtype=jnp.int32)[None, :, None]
    )
    spectral = implicit(analysed, degree, top_degree, mode_depth, diffusion)
    synth = jnp.einsum(
        "kpieqc,kpiy->pekqcy", spectral, basis, preferred_element_type=jnp.float32
    )
    gridded = jnp.stack(
        [quad_weights * (synth[0] + synth[1]), quad_weights * (synth[0] - synth[1])], axis=4
    ).astype(jnp.bfloat16)
    gridded = lax.all_to_all(gridded, "mem", 0, 0, tiled=True)
    gridded = gridded.reshape(padded, 2, channels, lat_count, band_rows)[:count_waves]
    gridded = jnp.transpose(gridded, (1, 3, 0, 2, 4))
    returned = lax.all_to_all(gridded, "lat", 1, 1, tiled=True)
    returned = returned.reshape(2 * total_waves, channels * band_rows)

    result = lax.dot_general(
        returned, table, (((0,), (1,)), ((), ())), preferred_element_type=jnp.float32
    )
    result = result * jnp.float32(1.0 / lon_count)
    return result.astype(jnp.bfloat16).reshape(members, fields, levels, band_rows, lon_count)


def solution(mesh):
    placed = (P("mem", None, None, "lat", None), P("lat", None, None, "mem"), P(), P(), P(), P())
    return jax.shard_map(
        shards,
        mesh=mesh,
        in_specs=placed,
        out_specs=P("mem", None, None, "lat", None),
        check_vma=False,
    )
```

```python
import math

import jax
import jax.numpy as jnp
from jax import lax
from jax.sharding import PartitionSpec as P


def fourier_table(waves, valid, lon_count):
    inner = 1 << (lon_count.bit_length() - 1) // 2
    outer = lon_count // inner
    step = jnp.float32(2.0 * math.pi / lon_count)
    waves = jnp.repeat(waves, 2)[None, :]
    valid = jnp.repeat(valid, 2)[None, :]
    even = (jnp.arange(waves.shape[1], dtype=jnp.int32) % 2 == 0)[None, :]
    phase_a = (jnp.arange(outer, dtype=jnp.int32)[:, None] * inner * waves) % lon_count
    phase_b = (jnp.arange(inner, dtype=jnp.int32)[:, None] * waves) % lon_count
    angle_a = phase_a.astype(jnp.float32) * step
    angle_b = phase_b.astype(jnp.float32) * step
    cos_a, sin_a = jnp.cos(angle_a), jnp.sin(angle_a)
    cos_b, sin_b = jnp.cos(angle_b), jnp.sin(angle_b)
    zero = jnp.zeros_like(cos_a)
    u = jnp.where(valid, jnp.where(even, cos_a, -sin_a), zero)
    v = jnp.where(valid, jnp.where(even, -sin_a, -cos_a), zero)
    table = u[:, None, :] * cos_b[None, :, :] + v[:, None, :] * sin_b[None, :, :]
    table = table.reshape(lon_count, -1).astype(jnp.bfloat16)
    return lax.optimization_barrier(table)


def implicit(values, degree, top_degree, mode_depth, diffusion):
    shape = values.shape
    levels = mode_depth.shape[0]
    values = values.reshape(shape[:-1] + (3, levels))
    degree_f = degree.astype(jnp.float32)
    scaled = (degree_f * (degree_f + 1.0) / (top_degree * (top_degree + 1.0)))[
        :, :, :, None, None, None
    ]
    vorticity = values[..., 0, :] / (1.0 + diffusion * scaled * scaled)
    damping = 1.0 / (1.0 + mode_depth * scaled)
    divergence = damping * (values[..., 1, :] - mode_depth * values[..., 2, :])
    height = damping * (scaled * values[..., 1, :] + values[..., 2, :])
    joined = jnp.stack([vorticity, divergence, height], axis=-2)
    return joined.reshape(shape).astype(jnp.bfloat16)


def shards(cotangent, legendre, wave_order, mode_depth, diffusion, quad_weights):
    members, fields, levels, band_rows, lon_count = cotangent.shape
    lat_count = lax.axis_size("lat")
    mem_count = lax.axis_size("mem")
    devices = lat_count * mem_count
    half_count = lat_count // 2
    total_waves = wave_order.shape[0]
    count_waves = total_waves // lat_count
    group = -(-count_waves // mem_count)
    padded = group * mem_count
    half_deg = legendre.shape[2]
    slab = legendre.shape[3]
    half_lat = slab * mem_count
    channels = fields * levels
    width = channels * band_rows
    top_degree = float(total_waves + 2 * half_deg - 2)
    lat_id = lax.axis_index("lat")
    mem_id = lax.axis_index("mem")

    basis = jnp.pad(legendre, ((0, padded - count_waves), (0, 0), (0, 0), (0, 0)))
    basis = basis.reshape(mem_count, group, 2, half_deg, slab)
    basis = lax.all_to_all(basis, "mem", 0, 0, tiled=True)
    basis = jnp.transpose(basis, (1, 2, 3, 0, 4)).reshape(group, 2, half_deg, half_lat)

    slot = (
        jnp.arange(mem_count, dtype=jnp.int32)[:, None, None] * group
        + jnp.arange(group, dtype=jnp.int32)[None, None, :]
    )
    slot = jnp.broadcast_to(slot, (mem_count, lat_count, group))
    index = jnp.arange(lat_count, dtype=jnp.int32)[None, :, None] * count_waves + slot
    valid = (slot < count_waves).reshape(-1)
    index = jnp.minimum(index, total_waves - 1).reshape(-1)
    column_waves = jnp.take(wave_order, index)
    table = fourier_table(column_waves, valid, lon_count)

    flattened = cotangent.reshape(width, lon_count)
    factor = jnp.where(column_waves == 0, 1.0, 2.0).astype(jnp.float32)
    factor = jnp.repeat(factor, 2)
    coeffs = lax.dot_general(
        table, flattened, (((0,), (1,)), ((), ())), preferred_element_type=jnp.float32
    )
    coeffs = (coeffs * factor[:, None]).astype(jnp.bfloat16)
    coeffs = coeffs.reshape(devices, group * 2 * width)
    received = lax.all_to_all(coeffs, ("mem", "lat"), 0, 0, tiled=True)
    received = received.reshape(mem_count, lat_count, group, 2, channels, band_rows)
    northern = received[:, :half_count].astype(jnp.float32)
    southern = received[:, half_count:].astype(jnp.float32)
    even_part = (northern + southern).astype(jnp.bfloat16)
    odd_part = (northern - southern).astype(jnp.bfloat16)
    parts = jnp.stack([even_part, odd_part], axis=0)
    parts = jnp.transpose(parts, (3, 0, 1, 4, 5, 2, 6)).reshape(
        group, 2, mem_count, 2, channels, half_lat
    )

    analysed = jnp.einsum(
        "kpiy,kpeqcy->kpieqc", basis, parts, preferred_element_type=jnp.float32
    )
    local = mem_id * group + jnp.arange(group, dtype=jnp.int32)
    index = jnp.minimum(lat_id * count_waves + local, total_waves - 1)
    own_waves = jnp.take(wave_order, index)
    degree = (
        own_waves[:, None, None]
        + 2 * jnp.arange(half_deg, dtype=jnp.int32)[None, None, :]
        + jnp.arange(2, dtype=jnp.int32)[None, :, None]
    )
    spectral = implicit(analysed, degree, top_degree, mode_depth, diffusion)
    synth = jnp.einsum(
        "kpieqc,kpiy->pekqcy", spectral, basis, preferred_element_type=jnp.float32
    )
    gridded = jnp.stack(
        [quad_weights * (synth[0] + synth[1]), quad_weights * (synth[0] - synth[1])], axis=1
    ).astype(jnp.bfloat16)
    gridded = gridded.reshape(mem_count, 2, group, 2, channels, half_count, band_rows)
    gridded = jnp.transpose(gridded, (0, 1, 5, 2, 3, 4, 6)).reshape(
        devices, group * 2 * width
    )
    returned = lax.all_to_all(gridded, ("mem", "lat"), 0, 0, tiled=True)
    returned = returned.reshape(devices * group * 2, width)

    result = lax.dot_general(
        returned, table, (((0,), (1,)), ((), ())), preferred_element_type=jnp.float32
    )
    result = result * jnp.float32(1.0 / lon_count)
    return result.astype(jnp.bfloat16).reshape(members, fields, levels, band_rows, lon_count)


def solution(mesh):
    placed = (P("mem", None, None, "lat", None), P("lat", None, None, "mem"), P(), P(), P(), P())
    return jax.shard_map(
        shards,
        mesh=mesh,
        in_specs=placed,
        out_specs=P("mem", None, None, "lat", None),
        check_vma=False,
    )
```

```python
import math

import jax
import jax.numpy as jnp
from jax import lax
from jax.sharding import PartitionSpec as P


def fourier_table(waves, lon_count):
    inner = 1 << (lon_count.bit_length() - 1) // 2
    outer = lon_count // inner
    step = jnp.float32(2.0 * math.pi / lon_count)
    even = (jnp.arange(waves.size, dtype=jnp.int32) % 2 == 0)[None, :]
    waves = waves.reshape(1, -1)
    phase_a = (jnp.arange(outer, dtype=jnp.int32)[:, None] * inner * waves) % lon_count
    phase_b = (jnp.arange(inner, dtype=jnp.int32)[:, None] * waves) % lon_count
    angle_a = phase_a.astype(jnp.float32) * step
    angle_b = phase_b.astype(jnp.float32) * step
    cos_a, sin_a = jnp.cos(angle_a), jnp.sin(angle_a)
    cos_b, sin_b = jnp.cos(angle_b), jnp.sin(angle_b)
    u = jnp.where(even, cos_a, -sin_a)
    v = jnp.where(even, -sin_a, -cos_a)
    table = u[:, None, :] * cos_b[None, :, :] + v[:, None, :] * sin_b[None, :, :]
    table = table.reshape(lon_count, -1).astype(jnp.bfloat16)
    return lax.optimization_barrier(table)


def implicit(values, degree, top_degree, mode_depth, diffusion):
    shape = values.shape
    levels = mode_depth.shape[0]
    values = values.reshape(shape[:-1] + (3, levels))
    degree_f = degree.astype(jnp.float32)
    scaled = (degree_f * (degree_f + 1.0) / (top_degree * (top_degree + 1.0)))[
        :, :, :, None, None, None
    ]
    vorticity = values[..., 0, :] / (1.0 + diffusion * scaled * scaled)
    damping = 1.0 / (1.0 + mode_depth * scaled)
    divergence = damping * (values[..., 1, :] - mode_depth * values[..., 2, :])
    height = damping * (scaled * values[..., 1, :] + values[..., 2, :])
    joined = jnp.stack([vorticity, divergence, height], axis=-2)
    return joined.reshape(shape).astype(jnp.bfloat16)


def shards(cotangent, legendre, wave_order, mode_depth, diffusion, quad_weights):
    members, fields, levels, band_rows, lon_count = cotangent.shape
    lat_count = lax.axis_size("lat")
    mem_count = lax.axis_size("mem")
    half_count = lat_count // 2
    total_waves = wave_order.shape[0]
    count_waves = total_waves // lat_count
    group = -(-count_waves // mem_count)
    padded = group * mem_count
    half_deg = legendre.shape[2]
    slab = legendre.shape[3]
    half_lat = slab * mem_count
    channels = fields * levels
    top_degree = float(total_waves + 2 * half_deg - 2)
    lat_id = lax.axis_index("lat")
    mem_id = lax.axis_index("mem")

    basis = jnp.pad(legendre, ((0, padded - count_waves), (0, 0), (0, 0), (0, 0)))
    basis = basis.reshape(mem_count, group, 2, half_deg, slab)
    basis = lax.all_to_all(basis, "mem", 0, 0, tiled=True)
    basis = jnp.transpose(basis, (1, 2, 3, 0, 4)).reshape(group, 2, half_deg, half_lat)

    column_waves = jnp.repeat(wave_order.reshape(lat_count, count_waves), 2, axis=1)
    table = fourier_table(column_waves, lon_count)
    flattened = cotangent.reshape(channels * band_rows, lon_count)
    factor = jnp.where(column_waves == 0, 1.0, 2.0).astype(jnp.float32).reshape(-1)
    coeffs = lax.dot_general(
        table, flattened, (((0,), (1,)), ((), ())), preferred_element_type=jnp.float32
    )
    coeffs = (coeffs * factor[:, None]).astype(jnp.bfloat16)
    coeffs = coeffs.reshape(lat_count, count_waves * 2, channels * band_rows)
    received = lax.all_to_all(coeffs, "lat", 0, 0, tiled=True)
    received = received.reshape(lat_count, count_waves, 2, channels, band_rows)
    northern = received[:half_count].astype(jnp.float32)
    southern = received[half_count:].astype(jnp.float32)
    even_part = (northern + southern).astype(jnp.bfloat16)
    odd_part = (northern - southern).astype(jnp.bfloat16)
    parts = jnp.stack([even_part, odd_part], axis=0)
    parts = jnp.pad(parts, ((0, 0), (0, 0), (0, padded - count_waves), (0, 0), (0, 0), (0, 0)))
    parts = jnp.transpose(parts, (2, 0, 3, 4, 1, 5)).reshape(
        mem_count, group, 2, 2, channels, half_lat
    )
    parts = lax.all_to_all(parts, "mem", 0, 0, tiled=True)

    analysed = jnp.einsum(
        "kpiy,ekpqcy->kpieqc", basis, parts, preferred_element_type=jnp.float32
    )
    local = mem_id * group + jnp.arange(group, dtype=jnp.int32)
    index = jnp.minimum(lat_id * count_waves + local, total_waves - 1)
    own_waves = jnp.take(wave_order, index)
    degree = (
        own_waves[:, None, None]
        + 2 * jnp.arange(half_deg, dtype=jnp.int32)[None, None, :]
        + jnp.arange(2, dtype=jnp.int32)[None, :, None]
    )
    spectral = implicit(analysed, degree, top_degree, mode_depth, diffusion)
    synth = jnp.einsum(
        "kpieqc,kpiy->pekqcy", spectral, basis, preferred_element_type=jnp.float32
    )
    gridded = jnp.stack(
        [quad_weights * (synth[0] + synth[1]), quad_weights * (synth[0] - synth[1])], axis=4
    ).astype(jnp.bfloat16)
    gridded = lax.all_to_all(gridded, "mem", 0, 0, tiled=True)
    gridded = gridded.reshape(padded, 2, channels, lat_count, band_rows)[:count_waves]
    gridded = jnp.transpose(gridded, (3, 0, 1, 2, 4))
    returned = lax.all_to_all(gridded, "lat", 0, 0, tiled=True)
    returned = returned.reshape(2 * total_waves, channels * band_rows)

    result = lax.dot_general(
        returned, table, (((0,), (1,)), ((), ())), preferred_element_type=jnp.float32
    )
    result = result * jnp.float32(1.0 / lon_count)
    return result.astype(jnp.bfloat16).reshape(members, fields, levels, band_rows, lon_count)


def solution(mesh):
    placed = (P("mem", None, None, "lat", None), P("lat", None, None, "mem"), P(), P(), P(), P())
    return jax.shard_map(
        shards,
        mesh=mesh,
        in_specs=placed,
        out_specs=P("mem", None, None, "lat", None),
        check_vma=False,
    )
```

```python
import math

import jax
import jax.numpy as jnp
from jax import lax
from jax.sharding import PartitionSpec as P


def fourier_table(wave_order, lon_count, part):
    inner = 1 << (lon_count.bit_length() - 1) // 2
    outer = lon_count // inner
    step = jnp.float32(2.0 * math.pi / lon_count)
    waves = wave_order[None, :]
    phase_a = (jnp.arange(outer, dtype=jnp.int32)[:, None] * inner * waves) % lon_count
    phase_b = (jnp.arange(inner, dtype=jnp.int32)[:, None] * waves) % lon_count
    angle_a = phase_a.astype(jnp.float32) * step
    angle_b = phase_b.astype(jnp.float32) * step
    cos_a, sin_a = jnp.cos(angle_a), jnp.sin(angle_a)
    cos_b, sin_b = jnp.cos(angle_b), jnp.sin(angle_b)
    if part == 0:
        u, v = cos_a, -sin_a
    else:
        u, v = -sin_a, -cos_a
    table = u[:, None, :] * cos_b[None, :, :] + v[:, None, :] * sin_b[None, :, :]
    table = table.reshape(lon_count, -1).astype(jnp.bfloat16)
    return lax.optimization_barrier(table)


def implicit(values, degree, top_degree, mode_depth, diffusion):
    shape = values.shape
    levels = mode_depth.shape[0]
    values = values.reshape(shape[:-1] + (3, levels))
    degree_f = degree.astype(jnp.float32)
    scaled = (degree_f * (degree_f + 1.0) / (top_degree * (top_degree + 1.0)))[
        :, :, :, None, None
    ]
    vorticity = values[..., 0, :] / (1.0 + diffusion * scaled * scaled)
    damping = 1.0 / (1.0 + mode_depth * scaled)
    divergence = damping * (values[..., 1, :] - mode_depth * values[..., 2, :])
    height = damping * (scaled * values[..., 1, :] + values[..., 2, :])
    joined = jnp.stack([vorticity, divergence, height], axis=-2)
    return joined.reshape(shape).astype(jnp.bfloat16)


def shards(cotangent, legendre, wave_order, mode_depth, diffusion, quad_weights):
    members, fields, levels, band_rows, lon_count = cotangent.shape
    lat_count = lax.axis_size("lat")
    mem_count = lax.axis_size("mem")
    half_count = lat_count // 2
    total_waves = wave_order.shape[0]
    count_waves = total_waves // lat_count
    group = -(-count_waves // mem_count)
    padded = group * mem_count
    half_deg = legendre.shape[2]
    slab = legendre.shape[3]
    half_lat = slab * mem_count
    channels = fields * levels
    width = channels * band_rows
    top_degree = float(total_waves + 2 * half_deg - 2)
    lat_id = lax.axis_index("lat")
    mem_id = lax.axis_index("mem")

    basis = jnp.pad(legendre, ((0, padded - count_waves), (0, 0), (0, 0), (0, 0)))
    basis = basis.reshape(mem_count, group, 2, half_deg, slab)
    basis = lax.all_to_all(basis, "mem", 0, 0, tiled=True)
    basis = jnp.transpose(basis, (1, 2, 3, 0, 4)).reshape(group, 2, half_deg, half_lat)

    local = mem_id * group + jnp.arange(group, dtype=jnp.int32)
    index = jnp.minimum(lat_id * count_waves + local, total_waves - 1)
    own_waves = jnp.take(wave_order, index)
    degree = (
        own_waves[:, None, None]
        + 2 * jnp.arange(half_deg, dtype=jnp.int32)[None, None, :]
        + jnp.arange(2, dtype=jnp.int32)[None, :, None]
    )
    flattened = cotangent.reshape(width, lon_count)
    factor = jnp.where(wave_order == 0, 1.0, 2.0).astype(jnp.float32)

    partials = []
    for part in range(2):
        table = fourier_table(wave_order, lon_count, part)
        coeffs = lax.dot_general(
            table, flattened, (((0,), (1,)), ((), ())), preferred_element_type=jnp.float32
        )
        coeffs = (coeffs * factor[:, None]).astype(jnp.bfloat16)
        coeffs = coeffs.reshape(lat_count, count_waves, width)
        received = lax.all_to_all(coeffs, "lat", 0, 0, tiled=True)
        received = received.reshape(lat_count, count_waves, channels, band_rows)
        northern = received[:half_count].astype(jnp.float32)
        southern = received[half_count:].astype(jnp.float32)
        even_part = (northern + southern).astype(jnp.bfloat16)
        odd_part = (northern - southern).astype(jnp.bfloat16)
        parts = jnp.stack([even_part, odd_part], axis=0)
        parts = jnp.pad(parts, ((0, 0), (0, 0), (0, padded - count_waves), (0, 0), (0, 0)))
        parts = jnp.transpose(parts, (2, 0, 3, 1, 4)).reshape(
            mem_count, group, 2, channels, half_lat
        )
        parts = lax.all_to_all(parts, "mem", 0, 0, tiled=True)

        analysed = jnp.einsum(
            "kpiy,ekpcy->kpiec", basis, parts, preferred_element_type=jnp.float32
        )
        spectral = implicit(analysed, degree, top_degree, mode_depth, diffusion)
        synth = jnp.einsum(
            "kpiec,kpiy->pekcy", spectral, basis, preferred_element_type=jnp.float32
        )
        gridded = jnp.stack(
            [quad_weights * (synth[0] + synth[1]), quad_weights * (synth[0] - synth[1])],
            axis=3,
        ).astype(jnp.bfloat16)
        gridded = lax.all_to_all(gridded, "mem", 0, 0, tiled=True)
        gridded = gridded.reshape(padded, channels, lat_count, band_rows)[:count_waves]
        gridded = jnp.transpose(gridded, (2, 0, 1, 3))
        returned = lax.all_to_all(gridded, "lat", 0, 0, tiled=True)
        returned = returned.reshape(total_waves, width)

        partials.append(
            lax.dot_general(
                returned, table, (((0,), (1,)), ((), ())), preferred_element_type=jnp.float32
            )
        )

    result = (partials[0] + partials[1]) * jnp.float32(1.0 / lon_count)
    return result.astype(jnp.bfloat16).reshape(members, fields, levels, band_rows, lon_count)


def solution(mesh):
    placed = (P("mem", None, None, "lat", None), P("lat", None, None, "mem"), P(), P(), P(), P())
    return jax.shard_map(
        shards,
        mesh=mesh,
        in_specs=placed,
        out_specs=P("mem", None, None, "lat", None),
        check_vma=False,
    )
```

```python
import math

import jax
import jax.numpy as jnp
from jax import lax
from jax.sharding import PartitionSpec as P


def fourier_table(waves, valid, lon_count):
    inner = 1 << (lon_count.bit_length() - 1) // 2
    outer = lon_count // inner
    step = jnp.float32(2.0 * math.pi / lon_count)
    even = (jnp.arange(waves.size, dtype=jnp.int32) % 2 == 0)[None, :]
    waves = waves.reshape(1, -1)
    valid = valid.reshape(1, -1)
    phase_a = (jnp.arange(outer, dtype=jnp.int32)[:, None] * inner * waves) % lon_count
    phase_b = (jnp.arange(inner, dtype=jnp.int32)[:, None] * waves) % lon_count
    angle_a = phase_a.astype(jnp.float32) * step
    angle_b = phase_b.astype(jnp.float32) * step
    cos_a, sin_a = jnp.cos(angle_a), jnp.sin(angle_a)
    cos_b, sin_b = jnp.cos(angle_b), jnp.sin(angle_b)
    zero = jnp.zeros_like(cos_a)
    u = jnp.where(valid, jnp.where(even, cos_a, -sin_a), zero)
    v = jnp.where(valid, jnp.where(even, -sin_a, -cos_a), zero)
    table = u[:, None, :] * cos_b[None, :, :] + v[:, None, :] * sin_b[None, :, :]
    table = table.reshape(lon_count, -1).astype(jnp.bfloat16)
    return lax.optimization_barrier(table)


def implicit(values, degree, top_degree, mode_depth, diffusion):
    shape = values.shape
    levels = mode_depth.shape[0]
    values = values.reshape(shape[:-1] + (3, levels))
    degree_f = degree.astype(jnp.float32)
    scaled = (degree_f * (degree_f + 1.0) / (top_degree * (top_degree + 1.0)))[
        :, :, :, None, None, None
    ]
    vorticity = values[..., 0, :] / (1.0 + diffusion * scaled * scaled)
    damping = 1.0 / (1.0 + mode_depth * scaled)
    divergence = damping * (values[..., 1, :] - mode_depth * values[..., 2, :])
    height = damping * (scaled * values[..., 1, :] + values[..., 2, :])
    joined = jnp.stack([vorticity, divergence, height], axis=-2)
    return joined.reshape(shape).astype(jnp.bfloat16)


def shards(cotangent, legendre, wave_order, mode_depth, diffusion, quad_weights):
    members, fields, levels, band_rows, lon_count = cotangent.shape
    lat_count = lax.axis_size("lat")
    mem_count = lax.axis_size("mem")
    half_count = lat_count // 2
    total_waves = wave_order.shape[0]
    count_waves = total_waves // lat_count
    group = -(-count_waves // mem_count)
    padded = group * mem_count
    half_deg = legendre.shape[2]
    slab = legendre.shape[3]
    half_lat = slab * mem_count
    channels = fields * levels
    width = channels * band_rows
    top_degree = float(total_waves + 2 * half_deg - 2)
    lat_id = lax.axis_index("lat")
    mem_id = lax.axis_index("mem")

    basis = jnp.pad(legendre, ((0, padded - count_waves), (0, 0), (0, 0), (0, 0)))
    basis = basis.reshape(mem_count, group, 2, half_deg, slab)
    basis = lax.all_to_all(basis, "mem", 0, 0, tiled=True)
    basis = jnp.transpose(basis, (1, 2, 3, 0, 4)).reshape(group, 2, half_deg, half_lat)

    slot = jnp.arange(padded, dtype=jnp.int32)
    index = jnp.arange(lat_count, dtype=jnp.int32)[:, None] * count_waves + slot[None, :]
    index = jnp.minimum(index, total_waves - 1)
    column_waves = jnp.repeat(jnp.take(wave_order, index), 2, axis=1)
    valid = jnp.broadcast_to((slot < count_waves)[None, :], (lat_count, padded))
    valid = jnp.repeat(valid, 2, axis=1)
    table = fourier_table(column_waves, valid, lon_count)
    flattened = cotangent.reshape(width, lon_count)
    factor = jnp.where(column_waves == 0, 1.0, 2.0).astype(jnp.float32).reshape(-1)
    coeffs = lax.dot_general(
        table, flattened, (((0,), (1,)), ((), ())), preferred_element_type=jnp.float32
    )
    coeffs = (coeffs * factor[:, None]).astype(jnp.bfloat16)
    coeffs = coeffs.reshape(lat_count, padded * 2, width)
    received = lax.all_to_all(coeffs, "lat", 0, 0, tiled=True)
    received = received.reshape(lat_count, mem_count, group, 2, channels, band_rows)
    northern = received[:half_count].astype(jnp.float32)
    southern = received[half_count:].astype(jnp.float32)
    even_part = (northern + southern).astype(jnp.bfloat16)
    odd_part = (northern - southern).astype(jnp.bfloat16)
    parts = jnp.stack([even_part, odd_part], axis=0)
    parts = jnp.transpose(parts, (2, 3, 0, 4, 5, 1, 6)).reshape(
        mem_count, group * 2 * 2 * channels, half_lat
    )
    parts = lax.all_to_all(parts, "mem", 0, 0, tiled=True)
    parts = parts.reshape(mem_count, group, 2, 2, channels, half_lat)

    analysed = jnp.einsum(
        "kpiy,ekpqcy->kpieqc", basis, parts, preferred_element_type=jnp.float32
    )
    local = mem_id * group + jnp.arange(group, dtype=jnp.int32)
    index = jnp.minimum(lat_id * count_waves + local, total_waves - 1)
    own_waves = jnp.take(wave_order, index)
    degree = (
        own_waves[:, None, None]
        + 2 * jnp.arange(half_deg, dtype=jnp.int32)[None, None, :]
        + jnp.arange(2, dtype=jnp.int32)[None, :, None]
    )
    spectral = implicit(analysed, degree, top_degree, mode_depth, diffusion)
    synth = jnp.einsum(
        "kpieqc,kpiy->pekqcy", spectral, basis, preferred_element_type=jnp.float32
    )
    gridded = jnp.stack(
        [quad_weights * (synth[0] + synth[1]), quad_weights * (synth[0] - synth[1])], axis=4
    ).astype(jnp.bfloat16)
    gridded = gridded.reshape(mem_count, group * 2 * channels, 2 * half_lat)
    gridded = lax.all_to_all(gridded, "mem", 0, 0, tiled=True)
    gridded = gridded.reshape(mem_count, group, 2, channels, lat_count, band_rows)
    gridded = jnp.transpose(gridded, (4, 0, 1, 2, 3, 5)).reshape(lat_count, padded * 2, width)
    returned = lax.all_to_all(gridded, "lat", 0, 0, tiled=True)
    returned = returned.reshape(lat_count * padded * 2, width)

    result = lax.dot_general(
        returned, table, (((0,), (1,)), ((), ())), preferred_element_type=jnp.float32
    )
    result = result * jnp.float32(1.0 / lon_count)
    return result.astype(jnp.bfloat16).reshape(members, fields, levels, band_rows, lon_count)


def solution(mesh):
    placed = (P("mem", None, None, "lat", None), P("lat", None, None, "mem"), P(), P(), P(), P())
    return jax.shard_map(
        shards,
        mesh=mesh,
        in_specs=placed,
        out_specs=P("mem", None, None, "lat", None),
        check_vma=False,
    )
```

```python
import math

import jax
import jax.numpy as jnp
from jax import lax
from jax.sharding import PartitionSpec as P


def fourier_table(waves, valid, lon_count):
    inner = 1 << (lon_count.bit_length() - 1) // 2
    outer = lon_count // inner
    step = jnp.float32(2.0 * math.pi / lon_count)
    even = (jnp.arange(waves.size, dtype=jnp.int32) % 2 == 0)[None, :]
    waves = waves.reshape(1, -1)
    valid = valid.reshape(1, -1)
    phase_a = (jnp.arange(outer, dtype=jnp.int32)[:, None] * inner * waves) % lon_count
    phase_b = (jnp.arange(inner, dtype=jnp.int32)[:, None] * waves) % lon_count
    angle_a = phase_a.astype(jnp.float32) * step
    angle_b = phase_b.astype(jnp.float32) * step
    cos_a, sin_a = jnp.cos(angle_a), jnp.sin(angle_a)
    cos_b, sin_b = jnp.cos(angle_b), jnp.sin(angle_b)
    zero = jnp.zeros_like(cos_a)
    u = jnp.where(valid, jnp.where(even, cos_a, -sin_a), zero)
    v = jnp.where(valid, jnp.where(even, -sin_a, -cos_a), zero)
    table = u[:, None, :] * cos_b[None, :, :] + v[:, None, :] * sin_b[None, :, :]
    table = table.reshape(lon_count, -1).astype(jnp.bfloat16)
    return lax.optimization_barrier(table)


def implicit(values, degree, top_degree, mode_depth, diffusion):
    shape = values.shape
    levels = mode_depth.shape[0]
    values = values.reshape(shape[:-1] + (3, levels))
    degree_f = degree.astype(jnp.float32)
    scaled = (degree_f * (degree_f + 1.0) / (top_degree * (top_degree + 1.0)))[
        :, :, :, None, None, None
    ]
    vorticity = values[..., 0, :] / (1.0 + diffusion * scaled * scaled)
    damping = 1.0 / (1.0 + mode_depth * scaled)
    divergence = damping * (values[..., 1, :] - mode_depth * values[..., 2, :])
    height = damping * (scaled * values[..., 1, :] + values[..., 2, :])
    joined = jnp.stack([vorticity, divergence, height], axis=-2)
    return joined.reshape(shape).astype(jnp.bfloat16)


def shards(cotangent, legendre, wave_order, mode_depth, diffusion, quad_weights):
    members, fields, levels, band_rows, lon_count = cotangent.shape
    lat_count = lax.axis_size("lat")
    mem_count = lax.axis_size("mem")
    half_count = lat_count // 2
    total_waves = wave_order.shape[0]
    count_waves = total_waves // lat_count
    group = -(-count_waves // mem_count)
    padded = group * mem_count
    half_deg = legendre.shape[2]
    slab = legendre.shape[3]
    half_lat = slab * mem_count
    channels = fields * levels
    width = channels * band_rows
    top_degree = float(total_waves + 2 * half_deg - 2)
    lat_id = lax.axis_index("lat")
    mem_id = lax.axis_index("mem")

    basis = jnp.pad(legendre, ((0, padded - count_waves), (0, 0), (0, 0), (0, 0)))
    basis = basis.reshape(mem_count, group, 2, half_deg, slab)
    basis = lax.all_to_all(basis, "mem", 0, 0, tiled=True)
    basis = jnp.transpose(basis, (1, 2, 3, 0, 4)).reshape(group, 2, half_deg, half_lat)

    slot = jnp.arange(padded, dtype=jnp.int32)
    index = jnp.arange(lat_count, dtype=jnp.int32)[:, None] * count_waves + slot[None, :]
    index = jnp.minimum(index, total_waves - 1)
    column_waves = jnp.repeat(jnp.take(wave_order, index), 2, axis=1)
    valid = jnp.broadcast_to((slot < count_waves)[None, :], (lat_count, padded))
    valid = jnp.repeat(valid, 2, axis=1)
    table = fourier_table(column_waves, valid, lon_count)
    flattened = cotangent.reshape(width, lon_count)
    factor = jnp.where(column_waves == 0, 1.0, 2.0).astype(jnp.float32).reshape(-1)
    coeffs = lax.dot_general(
        table, flattened, (((0,), (1,)), ((), ())), preferred_element_type=jnp.float32
    )
    coeffs = (coeffs * factor[:, None]).astype(jnp.bfloat16)
    coeffs = coeffs.reshape(lat_count, padded * 2, width)
    received = lax.all_to_all(coeffs, "lat", 0, 0, tiled=True)
    northern = received[:half_count].astype(jnp.float32)
    southern = received[half_count:].astype(jnp.float32)
    even_part = (northern + southern).astype(jnp.bfloat16)
    odd_part = (northern - southern).astype(jnp.bfloat16)
    parts = jnp.stack([even_part, odd_part], axis=0)
    parts = parts.reshape(2, half_count, mem_count, group, 2, channels, band_rows)
    parts = jnp.transpose(parts, (2, 3, 0, 4, 5, 1, 6)).reshape(
        mem_count, group * 2 * 2 * channels, half_lat
    )
    parts = lax.all_to_all(parts, "mem", 0, 0, tiled=True)
    parts = parts.reshape(mem_count, group, 2, 2, channels, half_lat)

    analysed = jnp.einsum(
        "kpiy,ekpqcy->kpieqc", basis, parts, preferred_element_type=jnp.float32
    )
    local = mem_id * group + jnp.arange(group, dtype=jnp.int32)
    index = jnp.minimum(lat_id * count_waves + local, total_waves - 1)
    own_waves = jnp.take(wave_order, index)
    degree = (
        own_waves[:, None, None]
        + 2 * jnp.arange(half_deg, dtype=jnp.int32)[None, None, :]
        + jnp.arange(2, dtype=jnp.int32)[None, :, None]
    )
    spectral = implicit(analysed, degree, top_degree, mode_depth, diffusion)
    synth = jnp.einsum(
        "kpieqc,kpiy->pekqcy", spectral, basis, preferred_element_type=jnp.float32
    )
    gridded = jnp.stack(
        [quad_weights * (synth[0] + synth[1]), quad_weights * (synth[0] - synth[1])], axis=4
    ).astype(jnp.bfloat16)
    gridded = gridded.reshape(mem_count, group * 2 * channels, 2 * half_lat)
    gridded = lax.all_to_all(gridded, "mem", 0, 0, tiled=True)
    gridded = gridded.reshape(mem_count, group, 2, channels, lat_count, band_rows)
    gridded = jnp.transpose(gridded, (4, 0, 1, 2, 3, 5)).reshape(lat_count, padded * 2, width)
    returned = lax.all_to_all(gridded, "lat", 0, 0, tiled=True)
    returned = returned.reshape(lat_count * padded * 2, width)

    result = lax.dot_general(
        returned, table, (((0,), (1,)), ((), ())), preferred_element_type=jnp.float32
    )
    result = result * jnp.float32(1.0 / lon_count)
    return result.astype(jnp.bfloat16).reshape(members, fields, levels, band_rows, lon_count)


def solution(mesh):
    placed = (P("mem", None, None, "lat", None), P("lat", None, None, "mem"), P(), P(), P(), P())
    return jax.shard_map(
        shards,
        mesh=mesh,
        in_specs=placed,
        out_specs=P("mem", None, None, "lat", None),
        check_vma=False,
    )
```

```python
import math

import jax
import jax.numpy as jnp
from jax import lax
from jax.sharding import PartitionSpec as P


def fourier_table(waves, valid, lon_count):
    inner = 1 << (lon_count.bit_length() - 1) // 2
    outer = lon_count // inner
    step = jnp.float32(2.0 * math.pi / lon_count)
    even = (jnp.arange(waves.size, dtype=jnp.int32) % 2 == 0)[None, :]
    waves = waves.reshape(1, -1)
    valid = valid.reshape(1, -1)
    phase_a = (jnp.arange(outer, dtype=jnp.int32)[:, None] * inner * waves) % lon_count
    phase_b = (jnp.arange(inner, dtype=jnp.int32)[:, None] * waves) % lon_count
    angle_a = phase_a.astype(jnp.float32) * step
    angle_b = phase_b.astype(jnp.float32) * step
    cos_a, sin_a = jnp.cos(angle_a), jnp.sin(angle_a)
    cos_b, sin_b = jnp.cos(angle_b), jnp.sin(angle_b)
    zero = jnp.zeros_like(cos_a)
    u = jnp.where(valid, jnp.where(even, cos_a, -sin_a), zero)
    v = jnp.where(valid, jnp.where(even, -sin_a, -cos_a), zero)
    table = u[:, None, :] * cos_b[None, :, :] + v[:, None, :] * sin_b[None, :, :]
    table = table.reshape(lon_count, -1).astype(jnp.bfloat16)
    return lax.optimization_barrier(table)


def inverse_table(waves, valid, lon_count):
    inner = math.gcd(lon_count, 128)
    outer = lon_count // inner
    step = jnp.float32(2.0 * math.pi / lon_count)
    even = (jnp.arange(waves.size, dtype=jnp.int32) % 2 == 0)[:, None]
    waves = waves.reshape(-1, 1)
    valid = valid.reshape(-1, 1)
    phase_a = (waves * inner * jnp.arange(outer, dtype=jnp.int32)[None, :]) % lon_count
    phase_b = (waves * jnp.arange(inner, dtype=jnp.int32)[None, :]) % lon_count
    angle_a = phase_a.astype(jnp.float32) * step
    angle_b = phase_b.astype(jnp.float32) * step
    cos_a, sin_a = jnp.cos(angle_a), jnp.sin(angle_a)
    cos_b, sin_b = jnp.cos(angle_b), jnp.sin(angle_b)
    zero = jnp.zeros_like(cos_a)
    u = jnp.where(valid, jnp.where(even, cos_a, -sin_a), zero)
    v = jnp.where(valid, jnp.where(even, -sin_a, -cos_a), zero)
    table = u[:, :, None] * cos_b[:, None, :] + v[:, :, None] * sin_b[:, None, :]
    return table.reshape(waves.shape[0], lon_count).astype(jnp.bfloat16)


def implicit(values, degree, top_degree, mode_depth, diffusion):
    shape = values.shape
    levels = mode_depth.shape[0]
    values = values.reshape(shape[:-1] + (3, levels))
    degree_f = degree.astype(jnp.float32)
    scaled = (degree_f * (degree_f + 1.0) / (top_degree * (top_degree + 1.0)))[
        :, :, :, None, None, None
    ]
    vorticity = values[..., 0, :] / (1.0 + diffusion * scaled * scaled)
    damping = 1.0 / (1.0 + mode_depth * scaled)
    divergence = damping * (values[..., 1, :] - mode_depth * values[..., 2, :])
    height = damping * (scaled * values[..., 1, :] + values[..., 2, :])
    joined = jnp.stack([vorticity, divergence, height], axis=-2)
    return joined.reshape(shape).astype(jnp.bfloat16)


def shards(cotangent, legendre, wave_order, mode_depth, diffusion, quad_weights):
    members, fields, levels, band_rows, lon_count = cotangent.shape
    lat_count = lax.axis_size("lat")
    mem_count = lax.axis_size("mem")
    half_count = lat_count // 2
    total_waves = wave_order.shape[0]
    count_waves = total_waves // lat_count
    group = -(-count_waves // mem_count)
    padded = group * mem_count
    half_deg = legendre.shape[2]
    slab = legendre.shape[3]
    half_lat = slab * mem_count
    channels = fields * levels
    width = channels * band_rows
    top_degree = float(total_waves + 2 * half_deg - 2)
    lat_id = lax.axis_index("lat")
    mem_id = lax.axis_index("mem")

    basis = jnp.pad(legendre, ((0, padded - count_waves), (0, 0), (0, 0), (0, 0)))
    basis = basis.reshape(mem_count, group, 2, half_deg, slab)
    basis = lax.all_to_all(basis, "mem", 0, 0, tiled=True)
    basis = jnp.transpose(basis, (1, 2, 3, 0, 4)).reshape(group, 2, half_deg, half_lat)

    slot = jnp.arange(padded, dtype=jnp.int32)
    column_waves = jnp.pad(
        wave_order.reshape(lat_count, count_waves), ((0, 0), (0, padded - count_waves))
    )
    column_waves = jnp.repeat(column_waves, 2, axis=1)
    valid = jnp.broadcast_to((slot < count_waves)[None, :], (lat_count, padded))
    valid = jnp.repeat(valid, 2, axis=1)
    table = fourier_table(column_waves, valid, lon_count)
    flattened = cotangent.reshape(width, lon_count)
    factor = jnp.where(column_waves == 0, 1.0, 2.0).astype(jnp.float32).reshape(-1)
    coeffs = lax.dot_general(
        table, flattened, (((0,), (1,)), ((), ())), preferred_element_type=jnp.float32
    )
    coeffs = (coeffs * factor[:, None]).astype(jnp.bfloat16)
    coeffs = coeffs.reshape(lat_count, padded * 2, width)
    received = lax.all_to_all(coeffs, "lat", 0, 0, tiled=True)
    northern = received[:half_count].astype(jnp.float32)
    southern = received[half_count:].astype(jnp.float32)
    even_part = (northern + southern).astype(jnp.bfloat16)
    odd_part = (northern - southern).astype(jnp.bfloat16)
    parts = jnp.stack([even_part, odd_part], axis=0)
    parts = parts.reshape(2, half_count, mem_count, group, 2, channels, band_rows)
    parts = jnp.transpose(parts, (2, 3, 0, 4, 5, 1, 6)).reshape(
        mem_count, group * 2 * 2 * channels, half_lat
    )
    parts = lax.all_to_all(parts, "mem", 0, 0, tiled=True)
    parts = parts.reshape(mem_count, group, 2, 2, channels, half_lat)

    analysed = jnp.einsum(
        "kpiy,ekpqcy->kpieqc", basis, parts, preferred_element_type=jnp.float32
    )
    local = mem_id * group + jnp.arange(group, dtype=jnp.int32)
    index = jnp.minimum(lat_id * count_waves + local, total_waves - 1)
    own_waves = jnp.take(wave_order, index)
    degree = (
        own_waves[:, None, None]
        + 2 * jnp.arange(half_deg, dtype=jnp.int32)[None, None, :]
        + jnp.arange(2, dtype=jnp.int32)[None, :, None]
    )
    spectral = implicit(analysed, degree, top_degree, mode_depth, diffusion)
    synth = jnp.einsum(
        "kpieqc,kpiy->pekqcy", spectral, basis, preferred_element_type=jnp.float32
    )
    gridded = jnp.stack(
        [quad_weights * (synth[0] + synth[1]), quad_weights * (synth[0] - synth[1])], axis=4
    ).astype(jnp.bfloat16)
    gridded = gridded.reshape(mem_count, group * 2 * channels, 2 * half_lat)
    gridded = lax.all_to_all(gridded, "mem", 0, 0, tiled=True)
    gridded = gridded.reshape(mem_count, group, 2, channels, lat_count, band_rows)
    gridded = jnp.transpose(gridded, (4, 0, 1, 2, 3, 5)).reshape(lat_count, padded * 2, width)
    returned = lax.all_to_all(gridded, "lat", 0, 0, tiled=True)
    returned = returned.reshape(lat_count * padded * 2, width)

    inverse = inverse_table(column_waves, valid, lon_count)
    result = lax.dot_general(
        returned, inverse, (((0,), (0,)), ((), ())), preferred_element_type=jnp.float32
    )
    result = result * jnp.float32(1.0 / lon_count)
    return result.astype(jnp.bfloat16).reshape(members, fields, levels, band_rows, lon_count)


def solution(mesh):
    placed = (P("mem", None, None, "lat", None), P("lat", None, None, "mem"), P(), P(), P(), P())
    return jax.shard_map(
        shards,
        mesh=mesh,
        in_specs=placed,
        out_specs=P("mem", None, None, "lat", None),
        check_vma=False,
    )
```

```python
import math

import jax
import jax.numpy as jnp
from jax import lax
from jax.sharding import PartitionSpec as P


def fourier_table(waves, valid, lon_count):
    inner = 1 << (lon_count.bit_length() - 1) // 2
    outer = lon_count // inner
    step = jnp.float32(2.0 * math.pi / lon_count)
    even = (jnp.arange(waves.size, dtype=jnp.int32) % 2 == 0)[None, :]
    waves = waves.reshape(1, -1)
    valid = valid.reshape(1, -1)
    phase_a = (jnp.arange(outer, dtype=jnp.int32)[:, None] * inner * waves) % lon_count
    phase_b = (jnp.arange(inner, dtype=jnp.int32)[:, None] * waves) % lon_count
    angle_a = phase_a.astype(jnp.float32) * step
    angle_b = phase_b.astype(jnp.float32) * step
    cos_a, sin_a = jnp.cos(angle_a), jnp.sin(angle_a)
    cos_b, sin_b = jnp.cos(angle_b), jnp.sin(angle_b)
    zero = jnp.zeros_like(cos_a)
    u = jnp.where(valid, jnp.where(even, cos_a, -sin_a), zero)
    v = jnp.where(valid, jnp.where(even, -sin_a, -cos_a), zero)
    table = u[:, None, :] * cos_b[None, :, :] + v[:, None, :] * sin_b[None, :, :]
    table = table.reshape(lon_count, -1).astype(jnp.bfloat16)
    return lax.optimization_barrier(table)


def inverse_table(waves, valid, lon_count):
    inner = math.gcd(lon_count, 128)
    outer = lon_count // inner
    step = jnp.float32(2.0 * math.pi / lon_count)
    even = (jnp.arange(waves.size, dtype=jnp.int32) % 2 == 0)[:, None]
    waves = waves.reshape(-1, 1)
    valid = valid.reshape(-1, 1)
    phase_a = (waves * inner * jnp.arange(outer, dtype=jnp.int32)[None, :]) % lon_count
    phase_b = (waves * jnp.arange(inner, dtype=jnp.int32)[None, :]) % lon_count
    angle_a = phase_a.astype(jnp.float32) * step
    angle_b = phase_b.astype(jnp.float32) * step
    cos_a, sin_a = jnp.cos(angle_a), jnp.sin(angle_a)
    cos_b, sin_b = jnp.cos(angle_b), jnp.sin(angle_b)
    zero = jnp.zeros_like(cos_a)
    u = jnp.where(valid, jnp.where(even, cos_a, -sin_a), zero)
    v = jnp.where(valid, jnp.where(even, -sin_a, -cos_a), zero)
    table = u[:, :, None] * cos_b[:, None, :] + v[:, :, None] * sin_b[:, None, :]
    return table.reshape(waves.shape[0], lon_count).astype(jnp.bfloat16)


def implicit(values, degree, top_degree, mode_depth, diffusion):
    shape = values.shape
    levels = mode_depth.shape[0]
    values = values.reshape(shape[:-1] + (3, levels))
    degree_f = degree.astype(jnp.float32)
    scaled = (degree_f * (degree_f + 1.0) / (top_degree * (top_degree + 1.0)))[
        :, :, :, None, None, None
    ]
    vorticity = values[..., 0, :] / (1.0 + diffusion * scaled * scaled)
    damping = 1.0 / (1.0 + mode_depth * scaled)
    divergence = damping * (values[..., 1, :] - mode_depth * values[..., 2, :])
    height = damping * (scaled * values[..., 1, :] + values[..., 2, :])
    joined = jnp.stack([vorticity, divergence, height], axis=-2)
    return joined.reshape(shape).astype(jnp.bfloat16)


def shards(cotangent, legendre, wave_order, mode_depth, diffusion, quad_weights):
    members, fields, levels, band_rows, lon_count = cotangent.shape
    lat_count = lax.axis_size("lat")
    mem_count = lax.axis_size("mem")
    half_count = lat_count // 2
    total_waves = wave_order.shape[0]
    count_waves = total_waves // lat_count
    group = -(-count_waves // mem_count)
    padded = group * mem_count
    half_deg = legendre.shape[2]
    slab = legendre.shape[3]
    half_lat = slab * mem_count
    channels = fields * levels
    width = channels * band_rows
    top_degree = float(total_waves + 2 * half_deg - 2)
    lat_id = lax.axis_index("lat")
    mem_id = lax.axis_index("mem")

    basis = jnp.pad(legendre, ((0, padded - count_waves), (0, 0), (0, 0), (0, 0)))
    basis = basis.reshape(mem_count, group, 2, half_deg, slab)
    basis = lax.all_to_all(basis, "mem", 0, 0, tiled=True)
    basis = jnp.transpose(basis, (1, 2, 3, 0, 4)).reshape(group, 2, half_deg, half_lat)

    slot = jnp.arange(padded, dtype=jnp.int32)
    column_waves = jnp.pad(
        wave_order.reshape(lat_count, count_waves), ((0, 0), (0, padded - count_waves))
    )
    column_waves = jnp.repeat(column_waves, 2, axis=1)
    valid = jnp.broadcast_to((slot < count_waves)[None, :], (lat_count, padded))
    valid = jnp.repeat(valid, 2, axis=1)
    table = fourier_table(column_waves, valid, lon_count)
    table, basis = lax.optimization_barrier((table, basis))
    flattened = cotangent.reshape(width, lon_count)
    factor = jnp.where(column_waves == 0, 1.0, 2.0).astype(jnp.float32).reshape(-1)
    coeffs = lax.dot_general(
        table, flattened, (((0,), (1,)), ((), ())), preferred_element_type=jnp.float32
    )
    coeffs = (coeffs * factor[:, None]).astype(jnp.bfloat16)
    coeffs = coeffs.reshape(lat_count, padded * 2, width)
    received = lax.all_to_all(coeffs, "lat", 0, 0, tiled=True)
    northern = received[:half_count].astype(jnp.float32)
    southern = received[half_count:].astype(jnp.float32)
    even_part = (northern + southern).astype(jnp.bfloat16)
    odd_part = (northern - southern).astype(jnp.bfloat16)
    parts = jnp.stack([even_part, odd_part], axis=0)
    parts = parts.reshape(2, half_count, mem_count, group, 2, channels, band_rows)
    parts = jnp.transpose(parts, (2, 3, 0, 4, 5, 1, 6)).reshape(
        mem_count, group * 2 * 2 * channels, half_lat
    )
    parts = lax.all_to_all(parts, "mem", 0, 0, tiled=True)
    parts = parts.reshape(mem_count, group, 2, 2, channels, half_lat)

    analysed = jnp.einsum(
        "kpiy,ekpqcy->kpieqc", basis, parts, preferred_element_type=jnp.float32
    )
    local = mem_id * group + jnp.arange(group, dtype=jnp.int32)
    index = jnp.minimum(lat_id * count_waves + local, total_waves - 1)
    own_waves = jnp.take(wave_order, index)
    degree = (
        own_waves[:, None, None]
        + 2 * jnp.arange(half_deg, dtype=jnp.int32)[None, None, :]
        + jnp.arange(2, dtype=jnp.int32)[None, :, None]
    )
    spectral = implicit(analysed, degree, top_degree, mode_depth, diffusion)
    synth = jnp.einsum(
        "kpieqc,kpiy->pekqcy", spectral, basis, preferred_element_type=jnp.float32
    )
    gridded = jnp.stack(
        [quad_weights * (synth[0] + synth[1]), quad_weights * (synth[0] - synth[1])], axis=4
    ).astype(jnp.bfloat16)
    gridded = gridded.reshape(mem_count, group * 2 * channels, 2 * half_lat)
    gridded = lax.all_to_all(gridded, "mem", 0, 0, tiled=True)
    gridded = gridded.reshape(mem_count, group, 2, channels, lat_count, band_rows)
    gridded = jnp.transpose(gridded, (4, 0, 1, 2, 3, 5)).reshape(lat_count, padded * 2, width)
    returned = lax.all_to_all(gridded, "lat", 0, 0, tiled=True)
    returned = returned.reshape(lat_count * padded * 2, width)

    inverse = inverse_table(column_waves, valid, lon_count)
    result = lax.dot_general(
        returned, inverse, (((0,), (0,)), ((), ())), preferred_element_type=jnp.float32
    )
    result = result * jnp.float32(1.0 / lon_count)
    return result.astype(jnp.bfloat16).reshape(members, fields, levels, band_rows, lon_count)


def solution(mesh):
    placed = (P("mem", None, None, "lat", None), P("lat", None, None, "mem"), P(), P(), P(), P())
    return jax.shard_map(
        shards,
        mesh=mesh,
        in_specs=placed,
        out_specs=P("mem", None, None, "lat", None),
        check_vma=False,
    )
```

```python
import math

import jax
import jax.numpy as jnp
from jax import lax
from jax.sharding import PartitionSpec as P


def fourier_table(waves, valid, lon_count):
    inner = 1 << (lon_count.bit_length() - 1) // 2
    outer = lon_count // inner
    step = jnp.float32(2.0 * math.pi / lon_count)
    even = (jnp.arange(waves.size, dtype=jnp.int32) % 2 == 0)[None, :]
    waves = waves.reshape(1, -1)
    valid = valid.reshape(1, -1)
    phase_a = (jnp.arange(outer, dtype=jnp.int32)[:, None] * inner * waves) % lon_count
    phase_b = (jnp.arange(inner, dtype=jnp.int32)[:, None] * waves) % lon_count
    angle_a = phase_a.astype(jnp.float32) * step
    angle_b = phase_b.astype(jnp.float32) * step
    cos_a, sin_a = jnp.cos(angle_a), jnp.sin(angle_a)
    cos_b, sin_b = jnp.cos(angle_b), jnp.sin(angle_b)
    zero = jnp.zeros_like(cos_a)
    u = jnp.where(valid, jnp.where(even, cos_a, -sin_a), zero)
    v = jnp.where(valid, jnp.where(even, -sin_a, -cos_a), zero)
    table = u[:, None, :] * cos_b[None, :, :] + v[:, None, :] * sin_b[None, :, :]
    table = table.reshape(lon_count, -1).astype(jnp.bfloat16)
    return lax.optimization_barrier(table)


def inverse_table(waves, valid, lon_count):
    inner = math.gcd(lon_count, 128)
    outer = lon_count // inner
    step = jnp.float32(2.0 * math.pi / lon_count)
    even = (jnp.arange(waves.size, dtype=jnp.int32) % 2 == 0)[:, None]
    waves = waves.reshape(-1, 1)
    valid = valid.reshape(-1, 1)
    phase_a = (waves * inner * jnp.arange(outer, dtype=jnp.int32)[None, :]) % lon_count
    phase_b = (waves * jnp.arange(inner, dtype=jnp.int32)[None, :]) % lon_count
    angle_a = phase_a.astype(jnp.float32) * step
    angle_b = phase_b.astype(jnp.float32) * step
    cos_a, sin_a = jnp.cos(angle_a), jnp.sin(angle_a)
    cos_b, sin_b = jnp.cos(angle_b), jnp.sin(angle_b)
    zero = jnp.zeros_like(cos_a)
    u = jnp.where(valid, jnp.where(even, cos_a, -sin_a), zero)
    v = jnp.where(valid, jnp.where(even, -sin_a, -cos_a), zero)
    table = u[:, :, None] * cos_b[:, None, :] + v[:, :, None] * sin_b[:, None, :]
    return table.reshape(waves.shape[0], lon_count).astype(jnp.bfloat16)


def implicit(values, degree, top_degree, mode_depth, diffusion):
    shape = values.shape
    levels = mode_depth.shape[0]
    values = values.reshape(shape[:-1] + (3, levels))
    degree_f = degree.astype(jnp.float32)
    scaled = (degree_f * (degree_f + 1.0) / (top_degree * (top_degree + 1.0)))[
        :, :, :, None, None, None
    ]
    vorticity = values[..., 0, :] / (1.0 + diffusion * scaled * scaled)
    damping = 1.0 / (1.0 + mode_depth * scaled)
    divergence = damping * (values[..., 1, :] - mode_depth * values[..., 2, :])
    height = damping * (scaled * values[..., 1, :] + values[..., 2, :])
    joined = jnp.stack([vorticity, divergence, height], axis=-2)
    return joined.reshape(shape).astype(jnp.bfloat16)


def shards(cotangent, legendre, wave_order, mode_depth, diffusion, quad_weights):
    members, fields, levels, band_rows, lon_count = cotangent.shape
    lat_count = lax.axis_size("lat")
    mem_count = lax.axis_size("mem")
    half_count = lat_count // 2
    total_waves = wave_order.shape[0]
    count_waves = total_waves // lat_count
    group = -(-count_waves // mem_count)
    padded = group * mem_count
    half_deg = legendre.shape[2]
    slab = legendre.shape[3]
    half_lat = slab * mem_count
    channels = fields * levels
    width = channels * band_rows
    top_degree = float(total_waves + 2 * half_deg - 2)
    lat_id = lax.axis_index("lat")
    mem_id = lax.axis_index("mem")

    basis = jnp.pad(legendre, ((0, padded - count_waves), (0, 0), (0, 0), (0, 0)))
    basis = basis.reshape(mem_count, group, 2, half_deg, slab)
    blocks = [lax.dynamic_index_in_dim(basis, mem_id, 0, keepdims=False)]
    for shift in range(1, mem_count):
        block = lax.dynamic_index_in_dim(basis, (mem_id + shift) % mem_count, 0, keepdims=False)
        pairs = [(i, (i + shift) % mem_count) for i in range(mem_count)]
        blocks.append(lax.ppermute(block, "mem", pairs))
    order = (mem_id - jnp.arange(mem_count, dtype=jnp.int32)) % mem_count
    basis = jnp.take(jnp.stack(blocks), order, axis=0)
    basis = jnp.transpose(basis, (1, 2, 3, 0, 4)).reshape(group, 2, half_deg, half_lat)

    slot = jnp.arange(padded, dtype=jnp.int32)
    column_waves = jnp.pad(
        wave_order.reshape(lat_count, count_waves), ((0, 0), (0, padded - count_waves))
    )
    column_waves = jnp.repeat(column_waves, 2, axis=1)
    valid = jnp.broadcast_to((slot < count_waves)[None, :], (lat_count, padded))
    valid = jnp.repeat(valid, 2, axis=1)
    table = fourier_table(column_waves, valid, lon_count)
    flattened = cotangent.reshape(width, lon_count)
    factor = jnp.where(column_waves == 0, 1.0, 2.0).astype(jnp.float32).reshape(-1)
    coeffs = lax.dot_general(
        table, flattened, (((0,), (1,)), ((), ())), preferred_element_type=jnp.float32
    )
    coeffs = (coeffs * factor[:, None]).astype(jnp.bfloat16)
    coeffs = coeffs.reshape(lat_count, padded * 2, width)
    received = lax.all_to_all(coeffs, "lat", 0, 0, tiled=True)
    northern = received[:half_count].astype(jnp.float32)
    southern = received[half_count:].astype(jnp.float32)
    even_part = (northern + southern).astype(jnp.bfloat16)
    odd_part = (northern - southern).astype(jnp.bfloat16)
    parts = jnp.stack([even_part, odd_part], axis=0)
    parts = parts.reshape(2, half_count, mem_count, group, 2, channels, band_rows)
    parts = jnp.transpose(parts, (2, 3, 0, 4, 5, 1, 6)).reshape(
        mem_count, group * 2 * 2 * channels, half_lat
    )
    parts = lax.all_to_all(parts, "mem", 0, 0, tiled=True)
    parts = parts.reshape(mem_count, group, 2, 2, channels, half_lat)

    analysed = jnp.einsum(
        "kpiy,ekpqcy->kpieqc", basis, parts, preferred_element_type=jnp.float32
    )
    local = mem_id * group + jnp.arange(group, dtype=jnp.int32)
    index = jnp.minimum(lat_id * count_waves + local, total_waves - 1)
    own_waves = jnp.take(wave_order, index)
    degree = (
        own_waves[:, None, None]
        + 2 * jnp.arange(half_deg, dtype=jnp.int32)[None, None, :]
        + jnp.arange(2, dtype=jnp.int32)[None, :, None]
    )
    spectral = implicit(analysed, degree, top_degree, mode_depth, diffusion)
    synth = jnp.einsum(
        "kpieqc,kpiy->pekqcy", spectral, basis, preferred_element_type=jnp.float32
    )
    gridded = jnp.stack(
        [quad_weights * (synth[0] + synth[1]), quad_weights * (synth[0] - synth[1])], axis=4
    ).astype(jnp.bfloat16)
    gridded = gridded.reshape(mem_count, group * 2 * channels, 2 * half_lat)
    gridded = lax.all_to_all(gridded, "mem", 0, 0, tiled=True)
    gridded = gridded.reshape(mem_count, group, 2, channels, lat_count, band_rows)
    gridded = jnp.transpose(gridded, (4, 0, 1, 2, 3, 5)).reshape(lat_count, padded * 2, width)
    returned = lax.all_to_all(gridded, "lat", 0, 0, tiled=True)
    returned = returned.reshape(lat_count * padded * 2, width)

    inverse = inverse_table(column_waves, valid, lon_count)
    result = lax.dot_general(
        returned, inverse, (((0,), (0,)), ((), ())), preferred_element_type=jnp.float32
    )
    result = result * jnp.float32(1.0 / lon_count)
    return result.astype(jnp.bfloat16).reshape(members, fields, levels, band_rows, lon_count)


def solution(mesh):
    placed = (P("mem", None, None, "lat", None), P("lat", None, None, "mem"), P(), P(), P(), P())
    return jax.shard_map(
        shards,
        mesh=mesh,
        in_specs=placed,
        out_specs=P("mem", None, None, "lat", None),
        check_vma=False,
    )
```

```python
import math

import jax
import jax.numpy as jnp
from jax import lax
from jax.sharding import PartitionSpec as P


def fourier_table(waves, valid, lon_count):
    inner = 1 << (lon_count.bit_length() - 1) // 2
    outer = lon_count // inner
    step = jnp.float32(2.0 * math.pi / lon_count)
    even = (jnp.arange(waves.size, dtype=jnp.int32) % 2 == 0)[None, :]
    waves = waves.reshape(1, -1)
    valid = valid.reshape(1, -1)
    phase_a = (jnp.arange(outer, dtype=jnp.int32)[:, None] * inner * waves) % lon_count
    phase_b = (jnp.arange(inner, dtype=jnp.int32)[:, None] * waves) % lon_count
    angle_a = phase_a.astype(jnp.float32) * step
    angle_b = phase_b.astype(jnp.float32) * step
    cos_a, sin_a = jnp.cos(angle_a), jnp.sin(angle_a)
    cos_b, sin_b = jnp.cos(angle_b), jnp.sin(angle_b)
    zero = jnp.zeros_like(cos_a)
    u = jnp.where(valid, jnp.where(even, cos_a, -sin_a), zero)
    v = jnp.where(valid, jnp.where(even, -sin_a, -cos_a), zero)
    table = u[:, None, :] * cos_b[None, :, :] + v[:, None, :] * sin_b[None, :, :]
    table = table.reshape(lon_count, -1).astype(jnp.bfloat16)
    return lax.optimization_barrier(table)


def inverse_table(waves, valid, lon_count):
    inner = math.gcd(lon_count, 128)
    outer = lon_count // inner
    step = jnp.float32(2.0 * math.pi / lon_count)
    even = (jnp.arange(waves.size, dtype=jnp.int32) % 2 == 0)[:, None]
    waves = waves.reshape(-1, 1)
    valid = valid.reshape(-1, 1)
    phase_a = (waves * inner * jnp.arange(outer, dtype=jnp.int32)[None, :]) % lon_count
    phase_b = (waves * jnp.arange(inner, dtype=jnp.int32)[None, :]) % lon_count
    angle_a = phase_a.astype(jnp.float32) * step
    angle_b = phase_b.astype(jnp.float32) * step
    cos_a, sin_a = jnp.cos(angle_a), jnp.sin(angle_a)
    cos_b, sin_b = jnp.cos(angle_b), jnp.sin(angle_b)
    zero = jnp.zeros_like(cos_a)
    u = jnp.where(valid, jnp.where(even, cos_a, -sin_a), zero)
    v = jnp.where(valid, jnp.where(even, -sin_a, -cos_a), zero)
    table = u[:, :, None] * cos_b[:, None, :] + v[:, :, None] * sin_b[:, None, :]
    return table.reshape(waves.shape[0], lon_count).astype(jnp.bfloat16)


def implicit(values, degree, top_degree, mode_depth, diffusion):
    shape = values.shape
    levels = mode_depth.shape[0]
    values = values.reshape(shape[:-1] + (3, levels))
    degree_f = degree.astype(jnp.float32)
    scaled = (degree_f * (degree_f + 1.0) / (top_degree * (top_degree + 1.0)))[
        :, :, :, None, None, None
    ]
    vorticity = values[..., 0, :] / (1.0 + diffusion * scaled * scaled)
    damping = 1.0 / (1.0 + mode_depth * scaled)
    divergence = damping * (values[..., 1, :] - mode_depth * values[..., 2, :])
    height = damping * (scaled * values[..., 1, :] + values[..., 2, :])
    joined = jnp.stack([vorticity, divergence, height], axis=-2)
    return joined.reshape(shape).astype(jnp.bfloat16)


def shards(cotangent, legendre, wave_order, mode_depth, diffusion, quad_weights):
    members, fields, levels, band_rows, lon_count = cotangent.shape
    lat_count = lax.axis_size("lat")
    mem_count = lax.axis_size("mem")
    half_count = lat_count // 2
    total_waves = wave_order.shape[0]
    count_waves = total_waves // lat_count
    group = -(-count_waves // mem_count)
    padded = group * mem_count
    half_deg = legendre.shape[2]
    slab = legendre.shape[3]
    half_lat = slab * mem_count
    channels = fields * levels
    width = channels * band_rows
    top_degree = float(total_waves + 2 * half_deg - 2)
    lat_id = lax.axis_index("lat")
    mem_id = lax.axis_index("mem")

    slot = jnp.arange(padded, dtype=jnp.int32)
    column_waves = jnp.pad(
        wave_order.reshape(lat_count, count_waves), ((0, 0), (0, padded - count_waves))
    )
    column_waves = jnp.repeat(column_waves, 2, axis=1)
    valid = jnp.broadcast_to((slot < count_waves)[None, :], (lat_count, padded))
    valid = jnp.repeat(valid, 2, axis=1)
    table = fourier_table(column_waves, valid, lon_count)
    flattened = cotangent.reshape(width, lon_count)
    factor = jnp.where(column_waves == 0, 1.0, 2.0).astype(jnp.float32).reshape(-1)
    coeffs = lax.dot_general(
        table, flattened, (((0,), (1,)), ((), ())), preferred_element_type=jnp.float32
    )
    coeffs = (coeffs * factor[:, None]).astype(jnp.bfloat16)
    coeffs, basis = lax.optimization_barrier((coeffs, legendre))
    basis = jnp.pad(basis, ((0, padded - count_waves), (0, 0), (0, 0), (0, 0)))
    basis = basis.reshape(mem_count, group, 2, half_deg, slab)
    blocks = [lax.dynamic_index_in_dim(basis, mem_id, 0, keepdims=False)]
    for shift in range(1, mem_count):
        block = lax.dynamic_index_in_dim(basis, (mem_id + shift) % mem_count, 0, keepdims=False)
        pairs = [(i, (i + shift) % mem_count) for i in range(mem_count)]
        blocks.append(lax.ppermute(block, "mem", pairs))
    order = (mem_id - jnp.arange(mem_count, dtype=jnp.int32)) % mem_count
    basis = jnp.take(jnp.stack(blocks), order, axis=0)
    basis = jnp.transpose(basis, (1, 2, 3, 0, 4)).reshape(group, 2, half_deg, half_lat)

    coeffs = coeffs.reshape(lat_count, padded * 2, width)
    received = lax.all_to_all(coeffs, "lat", 0, 0, tiled=True)
    northern = received[:half_count].astype(jnp.float32)
    southern = received[half_count:].astype(jnp.float32)
    even_part = (northern + southern).astype(jnp.bfloat16)
    odd_part = (northern - southern).astype(jnp.bfloat16)
    parts = jnp.stack([even_part, odd_part], axis=0)
    parts = parts.reshape(2, half_count, mem_count, group, 2, channels, band_rows)
    parts = jnp.transpose(parts, (2, 3, 0, 4, 5, 1, 6)).reshape(
        mem_count, group * 2 * 2 * channels, half_lat
    )
    parts = lax.all_to_all(parts, "mem", 0, 0, tiled=True)
    parts = parts.reshape(mem_count, group, 2, 2, channels, half_lat)

    analysed = jnp.einsum(
        "kpiy,ekpqcy->kpieqc", basis, parts, preferred_element_type=jnp.float32
    )
    local = mem_id * group + jnp.arange(group, dtype=jnp.int32)
    index = jnp.minimum(lat_id * count_waves + local, total_waves - 1)
    own_waves = jnp.take(wave_order, index)
    degree = (
        own_waves[:, None, None]
        + 2 * jnp.arange(half_deg, dtype=jnp.int32)[None, None, :]
        + jnp.arange(2, dtype=jnp.int32)[None, :, None]
    )
    spectral = implicit(analysed, degree, top_degree, mode_depth, diffusion)
    synth = jnp.einsum(
        "kpieqc,kpiy->pekqcy", spectral, basis, preferred_element_type=jnp.float32
    )
    gridded = jnp.stack(
        [quad_weights * (synth[0] + synth[1]), quad_weights * (synth[0] - synth[1])], axis=4
    ).astype(jnp.bfloat16)
    gridded = gridded.reshape(mem_count, group * 2 * channels, 2 * half_lat)
    gridded = lax.all_to_all(gridded, "mem", 0, 0, tiled=True)
    gridded = gridded.reshape(mem_count, group, 2, channels, lat_count, band_rows)
    gridded = jnp.transpose(gridded, (4, 0, 1, 2, 3, 5)).reshape(lat_count, padded * 2, width)
    returned = lax.all_to_all(gridded, "lat", 0, 0, tiled=True)
    returned = returned.reshape(lat_count * padded * 2, width)

    inverse = inverse_table(column_waves, valid, lon_count)
    result = lax.dot_general(
        returned, inverse, (((0,), (0,)), ((), ())), preferred_element_type=jnp.float32
    )
    result = result * jnp.float32(1.0 / lon_count)
    return result.astype(jnp.bfloat16).reshape(members, fields, levels, band_rows, lon_count)


def solution(mesh):
    placed = (P("mem", None, None, "lat", None), P("lat", None, None, "mem"), P(), P(), P(), P())
    return jax.shard_map(
        shards,
        mesh=mesh,
        in_specs=placed,
        out_specs=P("mem", None, None, "lat", None),
        check_vma=False,
    )
```

```python
import math

import jax
import jax.numpy as jnp
from jax import lax
from jax.sharding import PartitionSpec as P


def fourier_table(waves, valid, lon_count):
    inner = 1 << (lon_count.bit_length() - 1) // 2
    outer = lon_count // inner
    step = jnp.float32(2.0 * math.pi / lon_count)
    even = (jnp.arange(waves.size, dtype=jnp.int32) % 2 == 0)[None, :]
    waves = waves.reshape(1, -1)
    valid = valid.reshape(1, -1)
    phase_a = (jnp.arange(outer, dtype=jnp.int32)[:, None] * inner * waves) % lon_count
    phase_b = (jnp.arange(inner, dtype=jnp.int32)[:, None] * waves) % lon_count
    angle_a = phase_a.astype(jnp.float32) * step
    angle_b = phase_b.astype(jnp.float32) * step
    cos_a, sin_a = jnp.cos(angle_a), jnp.sin(angle_a)
    cos_b, sin_b = jnp.cos(angle_b), jnp.sin(angle_b)
    zero = jnp.zeros_like(cos_a)
    u = jnp.where(valid, jnp.where(even, cos_a, -sin_a), zero)
    v = jnp.where(valid, jnp.where(even, -sin_a, -cos_a), zero)
    table = u[:, None, :] * cos_b[None, :, :] + v[:, None, :] * sin_b[None, :, :]
    table = table.reshape(lon_count, -1).astype(jnp.bfloat16)
    return lax.optimization_barrier(table)


def inverse_table(waves, valid, lon_count):
    inner = math.gcd(lon_count, 128)
    outer = lon_count // inner
    step = jnp.float32(2.0 * math.pi / lon_count)
    even = (jnp.arange(waves.size, dtype=jnp.int32) % 2 == 0)[:, None]
    waves = waves.reshape(-1, 1)
    valid = valid.reshape(-1, 1)
    phase_a = (waves * inner * jnp.arange(outer, dtype=jnp.int32)[None, :]) % lon_count
    phase_b = (waves * jnp.arange(inner, dtype=jnp.int32)[None, :]) % lon_count
    angle_a = phase_a.astype(jnp.float32) * step
    angle_b = phase_b.astype(jnp.float32) * step
    cos_a, sin_a = jnp.cos(angle_a), jnp.sin(angle_a)
    cos_b, sin_b = jnp.cos(angle_b), jnp.sin(angle_b)
    zero = jnp.zeros_like(cos_a)
    u = jnp.where(valid, jnp.where(even, cos_a, -sin_a), zero)
    v = jnp.where(valid, jnp.where(even, -sin_a, -cos_a), zero)
    table = u[:, :, None] * cos_b[:, None, :] + v[:, :, None] * sin_b[:, None, :]
    return table.reshape(waves.shape[0], lon_count).astype(jnp.bfloat16)


def implicit(values, degree, top_degree, mode_depth, diffusion):
    shape = values.shape
    levels = mode_depth.shape[0]
    values = values.reshape(shape[:-1] + (3, levels))
    degree_f = degree.astype(jnp.float32)
    scaled = (degree_f * (degree_f + 1.0) / (top_degree * (top_degree + 1.0)))[
        :, :, :, None, None, None
    ]
    vorticity = values[..., 0, :] / (1.0 + diffusion * scaled * scaled)
    damping = 1.0 / (1.0 + mode_depth * scaled)
    divergence = damping * (values[..., 1, :] - mode_depth * values[..., 2, :])
    height = damping * (scaled * values[..., 1, :] + values[..., 2, :])
    joined = jnp.stack([vorticity, divergence, height], axis=-2)
    return joined.reshape(shape).astype(jnp.bfloat16)


def shards(cotangent, legendre, wave_order, mode_depth, diffusion, quad_weights):
    members, fields, levels, band_rows, lon_count = cotangent.shape
    lat_count = lax.axis_size("lat")
    mem_count = lax.axis_size("mem")
    half_count = lat_count // 2
    total_waves = wave_order.shape[0]
    count_waves = total_waves // lat_count
    group = -(-count_waves // mem_count)
    padded = group * mem_count
    half_deg = legendre.shape[2]
    slab = legendre.shape[3]
    half_lat = slab * mem_count
    channels = fields * levels
    width = channels * band_rows
    top_degree = float(total_waves + 2 * half_deg - 2)
    lat_id = lax.axis_index("lat")
    mem_id = lax.axis_index("mem")

    slot = jnp.arange(padded, dtype=jnp.int32)
    column_waves = jnp.pad(
        wave_order.reshape(lat_count, count_waves), ((0, 0), (0, padded - count_waves))
    )
    column_waves = jnp.repeat(column_waves, 2, axis=1)
    valid = jnp.broadcast_to((slot < count_waves)[None, :], (lat_count, padded))
    valid = jnp.repeat(valid, 2, axis=1)
    table = fourier_table(column_waves, valid, lon_count)
    flattened = cotangent.reshape(width, lon_count)
    factor = jnp.where(column_waves == 0, 1.0, 2.0).astype(jnp.float32).reshape(-1)
    coeffs = lax.dot_general(
        table, flattened, (((0,), (1,)), ((), ())), preferred_element_type=jnp.float32
    )
    coeffs = (coeffs * factor[:, None]).astype(jnp.bfloat16)
    coeffs = coeffs.reshape(lat_count, padded * 2, width)
    received = lax.all_to_all(coeffs, "lat", 0, 0, tiled=True)
    received, basis = lax.optimization_barrier((received, legendre))
    basis = jnp.pad(basis, ((0, padded - count_waves), (0, 0), (0, 0), (0, 0)))
    basis = basis.reshape(mem_count, group, 2, half_deg, slab)
    blocks = [lax.dynamic_index_in_dim(basis, mem_id, 0, keepdims=False)]
    for shift in range(1, mem_count):
        block = lax.dynamic_index_in_dim(basis, (mem_id + shift) % mem_count, 0, keepdims=False)
        pairs = [(i, (i + shift) % mem_count) for i in range(mem_count)]
        blocks.append(lax.ppermute(block, "mem", pairs))
    order = (mem_id - jnp.arange(mem_count, dtype=jnp.int32)) % mem_count
    basis = jnp.take(jnp.stack(blocks), order, axis=0)
    basis = jnp.transpose(basis, (1, 2, 3, 0, 4)).reshape(group, 2, half_deg, half_lat)

    northern = received[:half_count].astype(jnp.float32)
    southern = received[half_count:].astype(jnp.float32)
    even_part = (northern + southern).astype(jnp.bfloat16)
    odd_part = (northern - southern).astype(jnp.bfloat16)
    parts = jnp.stack([even_part, odd_part], axis=0)
    parts = parts.reshape(2, half_count, mem_count, group, 2, channels, band_rows)
    parts = jnp.transpose(parts, (2, 3, 0, 4, 5, 1, 6)).reshape(
        mem_count, group * 2 * 2 * channels, half_lat
    )
    parts = lax.all_to_all(parts, "mem", 0, 0, tiled=True)
    parts = parts.reshape(mem_count, group, 2, 2, channels, half_lat)

    analysed = jnp.einsum(
        "kpiy,ekpqcy->kpieqc", basis, parts, preferred_element_type=jnp.float32
    )
    local = mem_id * group + jnp.arange(group, dtype=jnp.int32)
    index = jnp.minimum(lat_id * count_waves + local, total_waves - 1)
    own_waves = jnp.take(wave_order, index)
    degree = (
        own_waves[:, None, None]
        + 2 * jnp.arange(half_deg, dtype=jnp.int32)[None, None, :]
        + jnp.arange(2, dtype=jnp.int32)[None, :, None]
    )
    spectral = implicit(analysed, degree, top_degree, mode_depth, diffusion)
    synth = jnp.einsum(
        "kpieqc,kpiy->pekqcy", spectral, basis, preferred_element_type=jnp.float32
    )
    gridded = jnp.stack(
        [quad_weights * (synth[0] + synth[1]), quad_weights * (synth[0] - synth[1])], axis=4
    ).astype(jnp.bfloat16)
    gridded = gridded.reshape(mem_count, group * 2 * channels, 2 * half_lat)
    gridded = lax.all_to_all(gridded, "mem", 0, 0, tiled=True)
    gridded = gridded.reshape(mem_count, group, 2, channels, lat_count, band_rows)
    gridded = jnp.transpose(gridded, (4, 0, 1, 2, 3, 5)).reshape(lat_count, padded * 2, width)
    returned = lax.all_to_all(gridded, "lat", 0, 0, tiled=True)
    returned = returned.reshape(lat_count * padded * 2, width)

    inverse = inverse_table(column_waves, valid, lon_count)
    result = lax.dot_general(
        returned, inverse, (((0,), (0,)), ((), ())), preferred_element_type=jnp.float32
    )
    result = result * jnp.float32(1.0 / lon_count)
    return result.astype(jnp.bfloat16).reshape(members, fields, levels, band_rows, lon_count)


def solution(mesh):
    placed = (P("mem", None, None, "lat", None), P("lat", None, None, "mem"), P(), P(), P(), P())
    return jax.shard_map(
        shards,
        mesh=mesh,
        in_specs=placed,
        out_specs=P("mem", None, None, "lat", None),
        check_vma=False,
    )
```

```python
import math

import jax
import jax.numpy as jnp
from jax import lax
from jax.sharding import PartitionSpec as P


def fourier_table(waves, valid, lon_count):
    inner = 1 << (lon_count.bit_length() - 1) // 2
    outer = lon_count // inner
    step = jnp.float32(2.0 * math.pi / lon_count)
    even = (jnp.arange(waves.size, dtype=jnp.int32) % 2 == 0)[None, :]
    waves = waves.reshape(1, -1)
    valid = valid.reshape(1, -1)
    phase_a = (jnp.arange(outer, dtype=jnp.int32)[:, None] * inner * waves) % lon_count
    phase_b = (jnp.arange(inner, dtype=jnp.int32)[:, None] * waves) % lon_count
    angle_a = phase_a.astype(jnp.float32) * step
    angle_b = phase_b.astype(jnp.float32) * step
    cos_a, sin_a = jnp.cos(angle_a), jnp.sin(angle_a)
    cos_b, sin_b = jnp.cos(angle_b), jnp.sin(angle_b)
    zero = jnp.zeros_like(cos_a)
    u = jnp.where(valid, jnp.where(even, cos_a, -sin_a), zero)
    v = jnp.where(valid, jnp.where(even, -sin_a, -cos_a), zero)
    table = u[:, None, :] * cos_b[None, :, :] + v[:, None, :] * sin_b[None, :, :]
    table = table.reshape(lon_count, -1).astype(jnp.bfloat16)
    return lax.optimization_barrier(table)


def inverse_table(waves, valid, lon_count):
    inner = math.gcd(lon_count, 128)
    outer = lon_count // inner
    step = jnp.float32(2.0 * math.pi / lon_count)
    even = (jnp.arange(waves.size, dtype=jnp.int32) % 2 == 0)[:, None]
    waves = waves.reshape(-1, 1)
    valid = valid.reshape(-1, 1)
    phase_a = (waves * inner * jnp.arange(outer, dtype=jnp.int32)[None, :]) % lon_count
    phase_b = (waves * jnp.arange(inner, dtype=jnp.int32)[None, :]) % lon_count
    angle_a = phase_a.astype(jnp.float32) * step
    angle_b = phase_b.astype(jnp.float32) * step
    cos_a, sin_a = jnp.cos(angle_a), jnp.sin(angle_a)
    cos_b, sin_b = jnp.cos(angle_b), jnp.sin(angle_b)
    zero = jnp.zeros_like(cos_a)
    u = jnp.where(valid, jnp.where(even, cos_a, -sin_a), zero)
    v = jnp.where(valid, jnp.where(even, -sin_a, -cos_a), zero)
    table = u[:, :, None] * cos_b[:, None, :] + v[:, :, None] * sin_b[:, None, :]
    return table.reshape(waves.shape[0], lon_count).astype(jnp.bfloat16)


def implicit(values, degree, top_degree, mode_depth, diffusion):
    shape = values.shape
    levels = mode_depth.shape[0]
    values = values.reshape(shape[:-1] + (3, levels))
    degree_f = degree.astype(jnp.float32)
    scaled = (degree_f * (degree_f + 1.0) / (top_degree * (top_degree + 1.0)))[
        :, :, :, None, None, None
    ]
    vorticity = values[..., 0, :] / (1.0 + diffusion * scaled * scaled)
    damping = 1.0 / (1.0 + mode_depth * scaled)
    divergence = damping * (values[..., 1, :] - mode_depth * values[..., 2, :])
    height = damping * (scaled * values[..., 1, :] + values[..., 2, :])
    joined = jnp.stack([vorticity, divergence, height], axis=-2)
    return joined.reshape(shape).astype(jnp.bfloat16)


def shards(cotangent, legendre, wave_order, mode_depth, diffusion, quad_weights):
    members, fields, levels, band_rows, lon_count = cotangent.shape
    lat_count = lax.axis_size("lat")
    mem_count = lax.axis_size("mem")
    half_count = lat_count // 2
    total_waves = wave_order.shape[0]
    count_waves = total_waves // lat_count
    group = -(-count_waves // mem_count)
    padded = group * mem_count
    half_deg = legendre.shape[2]
    slab = legendre.shape[3]
    half_lat = slab * mem_count
    channels = fields * levels
    width = channels * band_rows
    top_degree = float(total_waves + 2 * half_deg - 2)
    lat_id = lax.axis_index("lat")
    mem_id = lax.axis_index("mem")

    basis = jnp.pad(legendre, ((0, padded - count_waves), (0, 0), (0, 0), (0, 0)))
    basis = basis.reshape(mem_count, group, 2, half_deg, slab)
    basis = lax.all_to_all(basis, "mem", 0, 0, tiled=True)
    basis = jnp.transpose(basis, (1, 2, 3, 0, 4)).reshape(group, 2, half_deg, half_lat)

    slot = jnp.arange(padded, dtype=jnp.int32)
    column_waves = jnp.pad(
        wave_order.reshape(lat_count, count_waves), ((0, 0), (0, padded - count_waves))
    )
    column_waves = jnp.repeat(column_waves, 2, axis=1)
    valid = jnp.broadcast_to((slot < count_waves)[None, :], (lat_count, padded))
    valid = jnp.repeat(valid, 2, axis=1)
    table = fourier_table(column_waves, valid, lon_count)
    flattened = cotangent.reshape(width, lon_count)
    factor = jnp.where(column_waves == 0, 1.0, 2.0).astype(jnp.float32).reshape(-1)
    coeffs = lax.dot_general(
        table, flattened, (((0,), (1,)), ((), ())), preferred_element_type=jnp.float32
    )
    coeffs = (coeffs * factor[:, None]).astype(jnp.bfloat16)
    coeffs = coeffs.reshape(lat_count, padded * 2, width)[:, : 2 * count_waves]
    received = lax.all_to_all(coeffs, "lat", 0, 0, tiled=True)
    received = jnp.pad(received, ((0, 0), (0, 2 * (padded - count_waves)), (0, 0)))
    northern = received[:half_count].astype(jnp.float32)
    southern = received[half_count:].astype(jnp.float32)
    even_part = (northern + southern).astype(jnp.bfloat16)
    odd_part = (northern - southern).astype(jnp.bfloat16)
    parts = jnp.stack([even_part, odd_part], axis=0)
    parts = parts.reshape(2, half_count, mem_count, group, 2, channels, band_rows)
    parts = jnp.transpose(parts, (2, 3, 0, 4, 5, 1, 6)).reshape(
        mem_count, group * 2 * 2 * channels, half_lat
    )
    parts = lax.all_to_all(parts, "mem", 0, 0, tiled=True)
    parts = parts.reshape(mem_count, group, 2, 2, channels, half_lat)

    analysed = jnp.einsum(
        "kpiy,ekpqcy->kpieqc", basis, parts, preferred_element_type=jnp.float32
    )
    local = mem_id * group + jnp.arange(group, dtype=jnp.int32)
    index = jnp.minimum(lat_id * count_waves + local, total_waves - 1)
    own_waves = jnp.take(wave_order, index)
    degree = (
        own_waves[:, None, None]
        + 2 * jnp.arange(half_deg, dtype=jnp.int32)[None, None, :]
        + jnp.arange(2, dtype=jnp.int32)[None, :, None]
    )
    spectral = implicit(analysed, degree, top_degree, mode_depth, diffusion)
    synth = jnp.einsum(
        "kpieqc,kpiy->pekqcy", spectral, basis, preferred_element_type=jnp.float32
    )
    gridded = jnp.stack(
        [quad_weights * (synth[0] + synth[1]), quad_weights * (synth[0] - synth[1])], axis=4
    ).astype(jnp.bfloat16)
    gridded = gridded.reshape(mem_count, group * 2 * channels, 2 * half_lat)
    gridded = lax.all_to_all(gridded, "mem", 0, 0, tiled=True)
    gridded = gridded.reshape(mem_count, group, 2, channels, lat_count, band_rows)
    gridded = jnp.transpose(gridded, (4, 0, 1, 2, 3, 5)).reshape(lat_count, padded * 2, width)
    returned = lax.all_to_all(gridded[:, : 2 * count_waves], "lat", 0, 0, tiled=True)
    returned = jnp.pad(returned, ((0, 0), (0, 2 * (padded - count_waves)), (0, 0)))
    returned = returned.reshape(lat_count * padded * 2, width)

    inverse = inverse_table(column_waves, valid, lon_count)
    result = lax.dot_general(
        returned, inverse, (((0,), (0,)), ((), ())), preferred_element_type=jnp.float32
    )
    result = result * jnp.float32(1.0 / lon_count)
    return result.astype(jnp.bfloat16).reshape(members, fields, levels, band_rows, lon_count)


def solution(mesh):
    placed = (P("mem", None, None, "lat", None), P("lat", None, None, "mem"), P(), P(), P(), P())
    return jax.shard_map(
        shards,
        mesh=mesh,
        in_specs=placed,
        out_specs=P("mem", None, None, "lat", None),
        check_vma=False,
    )
```

```python
import math

import jax
import jax.numpy as jnp
from jax import lax
from jax.sharding import PartitionSpec as P


def fourier_table(waves, valid, lon_count):
    inner = 1 << (lon_count.bit_length() - 1) // 2
    outer = lon_count // inner
    step = jnp.float32(2.0 * math.pi / lon_count)
    even = (jnp.arange(waves.size, dtype=jnp.int32) % 2 == 0)[None, :]
    waves = waves.reshape(1, -1)
    valid = valid.reshape(1, -1)
    phase_a = (jnp.arange(outer, dtype=jnp.int32)[:, None] * inner * waves) % lon_count
    phase_b = (jnp.arange(inner, dtype=jnp.int32)[:, None] * waves) % lon_count
    angle_a = phase_a.astype(jnp.float32) * step
    angle_b = phase_b.astype(jnp.float32) * step
    cos_a, sin_a = jnp.cos(angle_a), jnp.sin(angle_a)
    cos_b, sin_b = jnp.cos(angle_b), jnp.sin(angle_b)
    u = jnp.where(even, cos_a, -sin_a)
    v = jnp.where(even, -sin_a, -cos_a)
    table = u[:, None, :] * cos_b[None, :, :] + v[:, None, :] * sin_b[None, :, :]
    table = table.reshape(lon_count, -1).astype(jnp.bfloat16)
    return lax.optimization_barrier(table)


def inverse_table(waves, valid, lon_count):
    inner = math.gcd(lon_count, 128)
    outer = lon_count // inner
    step = jnp.float32(2.0 * math.pi / lon_count)
    even = (jnp.arange(waves.size, dtype=jnp.int32) % 2 == 0)[:, None]
    waves = waves.reshape(-1, 1)
    valid = valid.reshape(-1, 1)
    phase_a = (waves * inner * jnp.arange(outer, dtype=jnp.int32)[None, :]) % lon_count
    phase_b = (waves * jnp.arange(inner, dtype=jnp.int32)[None, :]) % lon_count
    angle_a = phase_a.astype(jnp.float32) * step
    angle_b = phase_b.astype(jnp.float32) * step
    cos_a, sin_a = jnp.cos(angle_a), jnp.sin(angle_a)
    cos_b, sin_b = jnp.cos(angle_b), jnp.sin(angle_b)
    u = jnp.where(even, cos_a, -sin_a)
    v = jnp.where(even, -sin_a, -cos_a)
    table = u[:, :, None] * cos_b[:, None, :] + v[:, :, None] * sin_b[:, None, :]
    return table.reshape(waves.shape[0], lon_count).astype(jnp.bfloat16)


def implicit(values, degree, top_degree, mode_depth, diffusion):
    shape = values.shape
    levels = mode_depth.shape[0]
    values = values.reshape(shape[:-1] + (3, levels))
    degree_f = degree.astype(jnp.float32)
    scaled = (degree_f * (degree_f + 1.0) / (top_degree * (top_degree + 1.0)))[
        :, :, :, None, None, None
    ]
    vorticity = values[..., 0, :] / (1.0 + diffusion * scaled * scaled)
    damping = 1.0 / (1.0 + mode_depth * scaled)
    divergence = damping * (values[..., 1, :] - mode_depth * values[..., 2, :])
    height = damping * (scaled * values[..., 1, :] + values[..., 2, :])
    joined = jnp.stack([vorticity, divergence, height], axis=-2)
    return joined.reshape(shape).astype(jnp.bfloat16)


def shards(cotangent, legendre, wave_order, mode_depth, diffusion, quad_weights):
    members, fields, levels, band_rows, lon_count = cotangent.shape
    lat_count = lax.axis_size("lat")
    mem_count = lax.axis_size("mem")
    half_count = lat_count // 2
    total_waves = wave_order.shape[0]
    count_waves = total_waves // lat_count
    group = -(-count_waves // mem_count)
    padded = group * mem_count
    half_deg = legendre.shape[2]
    slab = legendre.shape[3]
    half_lat = slab * mem_count
    channels = fields * levels
    width = channels * band_rows
    top_degree = float(total_waves + 2 * half_deg - 2)
    lat_id = lax.axis_index("lat")
    mem_id = lax.axis_index("mem")

    basis = jnp.pad(legendre, ((0, padded - count_waves), (0, 0), (0, 0), (0, 0)))
    basis = basis.reshape(mem_count, group, 2, half_deg, slab)
    basis = lax.all_to_all(basis, "mem", 0, 0, tiled=True)
    basis = jnp.transpose(basis, (1, 2, 3, 0, 4)).reshape(group, 2, half_deg, half_lat)

    slot = jnp.arange(padded, dtype=jnp.int32)
    column_waves = jnp.pad(
        wave_order.reshape(lat_count, count_waves), ((0, 0), (0, padded - count_waves))
    )
    column_waves = jnp.repeat(column_waves, 2, axis=1)
    valid = jnp.broadcast_to((slot < count_waves)[None, :], (lat_count, padded))
    valid = jnp.repeat(valid, 2, axis=1)
    table = fourier_table(column_waves, valid, lon_count)
    flattened = cotangent.reshape(width, lon_count)
    factor = jnp.where(column_waves == 0, 1.0, 2.0).astype(jnp.float32).reshape(-1)
    coeffs = lax.dot_general(
        table, flattened, (((0,), (1,)), ((), ())), preferred_element_type=jnp.float32
    )
    coeffs = (coeffs * factor[:, None]).astype(jnp.bfloat16)
    coeffs = coeffs.reshape(lat_count, padded * 2, width)[:, : 2 * count_waves]
    received = lax.all_to_all(coeffs, "lat", 0, 0, tiled=True)
    received = jnp.pad(received, ((0, 0), (0, 2 * (padded - count_waves)), (0, 0)))
    northern = received[:half_count].astype(jnp.float32)
    southern = received[half_count:].astype(jnp.float32)
    even_part = (northern + southern).astype(jnp.bfloat16)
    odd_part = (northern - southern).astype(jnp.bfloat16)
    parts = jnp.stack([even_part, odd_part], axis=0)
    parts = parts.reshape(2, half_count, mem_count, group, 2, channels, band_rows)
    parts = jnp.transpose(parts, (2, 3, 0, 4, 5, 1, 6)).reshape(
        mem_count, group * 2 * 2 * channels, half_lat
    )
    parts = lax.all_to_all(parts, "mem", 0, 0, tiled=True)
    parts = parts.reshape(mem_count, group, 2, 2, channels, half_lat)

    analysed = jnp.einsum(
        "kpiy,ekpqcy->kpieqc", basis, parts, preferred_element_type=jnp.float32
    )
    local = mem_id * group + jnp.arange(group, dtype=jnp.int32)
    index = jnp.minimum(lat_id * count_waves + local, total_waves - 1)
    own_waves = jnp.take(wave_order, index)
    degree = (
        own_waves[:, None, None]
        + 2 * jnp.arange(half_deg, dtype=jnp.int32)[None, None, :]
        + jnp.arange(2, dtype=jnp.int32)[None, :, None]
    )
    spectral = implicit(analysed, degree, top_degree, mode_depth, diffusion)
    synth = jnp.einsum(
        "kpieqc,kpiy->pekqcy", spectral, basis, preferred_element_type=jnp.float32
    )
    gridded = jnp.stack(
        [quad_weights * (synth[0] + synth[1]), quad_weights * (synth[0] - synth[1])], axis=4
    ).astype(jnp.bfloat16)
    gridded = gridded.reshape(mem_count, group * 2 * channels, 2 * half_lat)
    gridded = lax.all_to_all(gridded, "mem", 0, 0, tiled=True)
    gridded = gridded.reshape(mem_count, group, 2, channels, lat_count, band_rows)
    gridded = jnp.transpose(gridded, (4, 0, 1, 2, 3, 5)).reshape(lat_count, padded * 2, width)
    returned = lax.all_to_all(gridded[:, : 2 * count_waves], "lat", 0, 0, tiled=True)
    returned = jnp.pad(returned, ((0, 0), (0, 2 * (padded - count_waves)), (0, 0)))
    returned = returned.reshape(lat_count * padded * 2, width)

    inverse = inverse_table(column_waves, valid, lon_count)
    result = lax.dot_general(
        returned, inverse, (((0,), (0,)), ((), ())), preferred_element_type=jnp.float32
    )
    result = result * jnp.float32(1.0 / lon_count)
    return result.astype(jnp.bfloat16).reshape(members, fields, levels, band_rows, lon_count)


def solution(mesh):
    placed = (P("mem", None, None, "lat", None), P("lat", None, None, "mem"), P(), P(), P(), P())
    return jax.shard_map(
        shards,
        mesh=mesh,
        in_specs=placed,
        out_specs=P("mem", None, None, "lat", None),
        check_vma=False,
    )
```
